32 devices in a mesh: arrays: 2 (over y), elem: 4 (over z), gate: 2 (over x), pol: 2 (over core).
Axes of the slice: x: 2, y: 2, z: 4, core: 2. Of those that a mesh axis runs over, the one named last changes fastest.
Arguments:
- signal: bfloat16 [4, 2, 16384, 1024], P('arrays', 'pol', 'elem', 'gate'), parts along dimension 0, may hold values from -170 to 170
- weights: bfloat16 [4, 2, 1024, 16384], P('arrays', 'pol', None, 'elem'), parts along dimension 0, may hold values from -0.0625 to 0.0625
Outputs:
- moments: float32 [4, 4, 1024, 16], P(None, ('arrays', 'pol'), 'elem', 'gate'), parts along dimension 1
- polar: float32 [2, 2048, 16], P('pol', ('arrays', 'elem'), 'gate'), parts along dimension 1
The draws below stay inside these ranges and needn't reach their ends.
There are 2 independent parts, one for each index of `arrays`. The reference program is written for one: setup_inputs(seed, part) draws one part's arguments, and reference() takes and returns one part's arrays. A program takes and returns all parts, laid end to end along the dimension named above; each array names one. Nothing has to cross between parts.
All inputs are finite; a program needn't handle non-finite values.
Results may differ from the reference program's by a relative error of at most 0.0003.
Values sent between devices are 32-bit elements; how exact they have to be, the bound alone decides.
No kernel may reach another device: no remote copies, remote signals or barrier semaphores. Data moves between devices by JAX's collectives and lax.ppermute only.
A program may use at most 128 MiB of HBM per device.

```python
import math
import jax
import jax.numpy as jnp
from jax import lax

E = 16384
BEAMS = 1024
PULSES = 64
GATES = 16
ROWS = 1024
POLS = 2
N_ELEM = 4


def draw_signal(key, part):
    keys = jax.random.split(key, 5)
    shape = (2, 2, E, GATES, PULSES + 1)
    base = jax.random.truncated_normal(keys[0], -4.0, 4.0, shape, jnp.float32)
    first = base[:, 0]
    second = 0.8 * first + 0.6 * base[:, 1]
    corr = jax.random.uniform(keys[1], (GATES, 1), jnp.float32, 0.0, 1.0)
    angle = jax.random.uniform(keys[2], (GATES, 1), jnp.float32, -math.pi, math.pi)
    cosine = jnp.cos(angle)
    sine = jnp.sin(angle)

    def mixed(noise):
        current = noise[..., 1:]
        before = noise[..., :-1]
        real = current[0] + corr * (cosine * before[0] - sine * before[1])
        imag = current[1] + corr * (sine * before[0] + cosine * before[1])
        return jnp.stack([real, imag]) / jnp.sqrt(1.0 + corr * corr)
    pulse_scale = jnp.exp(jax.random.uniform(keys[3], (GATES, PULSES), jnp.float32, 0.0, math.log(10.0)))
    elem_scale = jnp.exp(jax.random.uniform(keys[4], (E, 1, 1), jnp.float32, 0.0, math.log(10.0)))
    values = jnp.stack([mixed(first), mixed(second)], axis=1) * elem_scale * pulse_scale * 0.1
    return values.reshape(2, POLS, E, GATES * PULSES).astype(jnp.bfloat16)


def raised(result, own_key, source, target, parts, factor):
    owner, partner = [(jnp.arange(result.shape[position]) // (result.shape[position] // parts)).reshape([-1 if axis == position else 1 for axis in range(result.ndim)]) for position in (source, target)]
    chosen = jax.random.permutation(own_key, parts)[partner]
    strong = (owner == chosen) | (owner == (partner + parts // 2) % parts)
    return jnp.where(strong, factor * result, result)


def steps_of(rng, extent, cuts, smallest, high):
    level, own = 1.0, jax.random.fold_in(rng, 6)
    for dim, blocks in cuts:
        heights = jnp.exp(jax.random.uniform(jax.random.fold_in(own, dim), (blocks,), jnp.float32, smallest / len(cuts), high / len(cuts)))
        level = level * jnp.repeat(heights, extent[dim] // blocks).reshape([-1 if axis == dim else 1 for axis in range(len(extent))])
    return level


def noise_with(rng, extent, spread, limit, cuts, heavy, held_as=jnp.bfloat16):
    array = spread * jax.random.normal(rng, extent, jnp.float32)
    if cuts:
        array = array * steps_of(rng, extent, cuts, -0.22, 0.18)
    return jnp.clip(raised(array, jax.random.fold_in(rng, 3), *heavy), -limit, limit).astype(held_as)


def setup_inputs(seed: int = 0, part: int = 0) -> dict:
    streams_of = jax.random.split(jax.random.key(seed), 3)
    part_splits = jax.random.split(jax.random.fold_in(streams_of[2], part), 3)
    signal = draw_signal(jax.random.fold_in(jax.random.fold_in(streams_of[2], part), 71), part)
    weights = noise_with(part_splits[1], (2, POLS, BEAMS, E), E ** -0.5, 0.0625, ((1, 2), (3, 4)), (3, 2, 4, 2.0))
    return dict(signal=signal, weights=weights)


def form_beams(signal_pol, weights_pol):
    block = E // N_ELEM
    width = ROWS

    def step(total, index):
        start = (index * block).astype(jnp.int32)
        w_block = lax.dynamic_slice_in_dim(weights_pol, start, block, 2)
        x_block = lax.dynamic_slice_in_dim(signal_pol, start, block, 1)
        stacked = w_block.reshape(2 * BEAMS, block).astype(jnp.float32)
        columns = jnp.concatenate([x_block[0], x_block[1]], axis=1).astype(jnp.float32)
        product = jnp.dot(stacked, columns, preferred_element_type=jnp.float32, precision=lax.Precision.HIGHEST)
        real = product[:BEAMS, :width] + product[BEAMS:, width:]
        imag = product[:BEAMS, width:] - product[BEAMS:, :width]
        partial_sum = jnp.concatenate([real, imag], axis=1)
        return (total + partial_sum, None)
    start_total = jnp.zeros((BEAMS, 2 * width), jnp.float32)
    total, unused = lax.scan(step, start_total, jnp.arange(N_ELEM, dtype=jnp.int32))
    real = total[:, :width].reshape(BEAMS, GATES, PULSES)
    imag = total[:, width:].reshape(BEAMS, GATES, PULSES)
    return (real, imag)

def lag_stats(real, imag):
    zero_lag = lax.optimization_barrier(jnp.mean(real * real + imag * imag, axis=-1))
    lag_re = lax.optimization_barrier(jnp.sum(real[..., :-1] * real[..., 1:] + imag[..., :-1] * imag[..., 1:], axis=-1)) / (PULSES - 1)
    lag_im = lax.optimization_barrier(jnp.sum(real[..., :-1] * imag[..., 1:] - imag[..., :-1] * real[..., 1:], axis=-1)) / (PULSES - 1)
    return (zero_lag, lag_re, lag_im)

def pair_stats(first, second):
    power_h = lax.optimization_barrier(jnp.mean(first[0] * first[0] + first[1] * first[1], axis=-1))
    power_v = lax.optimization_barrier(jnp.mean(second[0] * second[0] + second[1] * second[1], axis=-1))
    cross_re = lax.optimization_barrier(jnp.mean(first[0] * second[0] + first[1] * second[1], axis=-1))
    cross_im = lax.optimization_barrier(jnp.mean(first[0] * second[1] - first[1] * second[0], axis=-1))
    return (power_h, power_v, cross_re, cross_im)

def smooth(stats):
    padded = jnp.pad(stats, ((0, 0), (0, 0), (1, 1)))
    return (padded[..., :-2] + 2.0 * padded[..., 1:-1] + padded[..., 2:]) * 0.25

def finish_moments(zero_lag, lag_re, lag_im):
    magnitude = jnp.sqrt(lag_re * lag_re + lag_im * lag_im)
    floor_mag = jnp.maximum(magnitude, 0.25 * zero_lag)
    return jnp.stack([10.0 * jnp.log10(zero_lag + 1e-06), lag_re / floor_mag, lag_im / floor_mag, jnp.log(zero_lag / floor_mag)])

def reference(signal, weights):
    series = []
    for channel in range(2):
        series.append(form_beams(signal[:, channel], weights[:, channel]))
    moment_list = []
    for channel in range(2):
        real, imag = series[channel]
        zero_lag, lag_re, lag_im = lag_stats(real, imag)
        smoothed = smooth(jnp.stack([zero_lag, lag_re, lag_im]))
        moment_list.append(finish_moments(smoothed[0], smoothed[1], smoothed[2]))
    moments = jnp.stack(moment_list, axis=1)
    first = jnp.stack(series[0])
    second = jnp.stack(series[1])
    power_h, power_v, cross_re, cross_im = pair_stats(first, second)
    smoothed = smooth(jnp.stack([power_h, power_v, cross_re, cross_im]))
    zdr = 10.0 * jnp.log10((smoothed[0] + 1e-06) / (smoothed[1] + 1e-06))
    corr = jnp.sqrt(smoothed[2] * smoothed[2] + smoothed[3] * smoothed[3]) / jnp.sqrt(smoothed[0] * smoothed[1])
    return (moments, jnp.stack([zdr, corr]))
```

```python
import jax
import jax.numpy as jnp
from jax import lax
from jax.sharding import PartitionSpec as P

PULSES = 64
CHUNKS = 4


def swapped(value, axis, bit):
    mask = 2**bit
    pairs = [(source, source ^ mask) for source in range(lax.axis_size(axis))]
    return lax.ppermute(value, axis, pairs)


def with_halo(block, axis, dim):
    count = lax.axis_size(axis)
    first = lax.slice_in_dim(block, 0, 1, axis=dim)
    last = lax.slice_in_dim(block, block.shape[dim] - 1, None, axis=dim)
    index = lax.axis_index(axis)
    if count == 2:
        sent = jnp.where(index == 0, last, first)
        got = lax.ppermute(sent, axis, [(0, 1), (1, 0)])
        zero = jnp.zeros_like(got)
        low = jnp.where(index == 0, zero, got)
        high = jnp.where(index == 0, got, zero)
    else:
        forward = [(i, i + 1) for i in range(count - 1)]
        backward = [(target, source) for source, target in forward]
        low = lax.ppermute(last, axis, forward)
        high = lax.ppermute(first, axis, backward)
    return jnp.concatenate([low, block, high], axis=dim)


def lag_stats(real, imag):
    zero_lag = jnp.mean(real * real + imag * imag, axis=-1)
    lag_re = jnp.sum(real[..., :-1] * real[..., 1:] + imag[..., :-1] * imag[..., 1:], axis=-1) / (
        PULSES - 1
    )
    lag_im = jnp.sum(real[..., :-1] * imag[..., 1:] - imag[..., :-1] * real[..., 1:], axis=-1) / (
        PULSES - 1
    )
    return (zero_lag, lag_re, lag_im)


def pair_stats(first, second):
    power_h = jnp.mean(first[0] * first[0] + first[1] * first[1], axis=-1)
    power_v = jnp.mean(second[0] * second[0] + second[1] * second[1], axis=-1)
    cross_re = jnp.mean(first[0] * second[0] + first[1] * second[1], axis=-1)
    cross_im = jnp.mean(first[0] * second[1] - first[1] * second[0], axis=-1)
    return (power_h, power_v, cross_re, cross_im)


def chunk_stats(summed, gates):
    count = summed.shape[1]
    real = summed[0].reshape(count, gates, PULSES)
    imag = summed[1].reshape(count, gates, PULSES)
    zero_lag, lag_re, lag_im = lag_stats(real, imag)
    series = jnp.stack([real, imag])
    pol_index = lax.axis_index("pol")
    other = swapped(series, "pol", 0)
    first = jnp.where(pol_index == 0, series, other)
    second = jnp.where(pol_index == 0, other, series)
    pair = jnp.stack(pair_stats(first, second))
    return jnp.concatenate([jnp.stack([zero_lag, lag_re, lag_im]), pair], axis=0)


def on_device(signal, weights):
    n_elem = lax.axis_size("elem")
    samples = signal.shape[3]
    gates = samples // PULSES
    beams = weights.shape[2]
    elems = weights.shape[3]
    local = beams // n_elem
    chunks = CHUNKS
    while chunks > 1 and local % (chunks * 8):
        chunks //= 2
    per = local // chunks
    w = weights[:, 0].reshape(2, n_elem, chunks, per, elems)
    x_re = signal[0, 0]
    x_im = signal[1, 0]
    parts = []
    for j in range(chunks):
        rows = w[:, :, j].reshape(2 * n_elem * per, elems)
        p_re = jnp.dot(rows, x_re, preferred_element_type=jnp.float32).reshape(2, n_elem * per, samples)
        p_im = jnp.dot(rows, x_im, preferred_element_type=jnp.float32).reshape(2, n_elem * per, samples)
        combined = jnp.stack([p_re[0] + p_im[1], p_im[0] - p_re[1]])
        summed = lax.psum_scatter(combined, "elem", scatter_dimension=1, tiled=True)
        parts.append(chunk_stats(summed, gates))
    stats = jnp.concatenate(parts, axis=1)
    padded = with_halo(stats, "gate", 2)
    smoothed = (padded[..., :-2] + 2.0 * padded[..., 1:-1] + padded[..., 2:]) * 0.25
    power = smoothed[0]
    magnitude = jnp.sqrt(smoothed[1] * smoothed[1] + smoothed[2] * smoothed[2])
    floor_mag = jnp.maximum(magnitude, 0.25 * power)
    moments = jnp.stack(
        [
            10.0 * jnp.log10(power + 1e-06),
            smoothed[1] / floor_mag,
            smoothed[2] / floor_mag,
            jnp.log(power / floor_mag),
        ]
    )
    zdr = 10.0 * jnp.log10((smoothed[3] + 1e-06) / (smoothed[4] + 1e-06))
    corr = jnp.sqrt(smoothed[5] * smoothed[5] + smoothed[6] * smoothed[6]) / jnp.sqrt(
        smoothed[3] * smoothed[4]
    )
    pol_index = lax.axis_index("pol")
    polar = jnp.where(pol_index == 0, zdr, corr)
    return (moments[:, None], polar[None])


def solution(mesh):
    return jax.shard_map(
        on_device,
        mesh=mesh,
        in_specs=(P("arrays", "pol", "elem", "gate"), P("arrays", "pol", None, "elem")),
        out_specs=(
            P(None, ("arrays", "pol"), "elem", "gate"),
            P("pol", ("arrays", "elem"), "gate"),
        ),
        check_vma=False,
    )
```

```python
import jax
import jax.numpy as jnp
from jax import lax
from jax.experimental import pallas as pl
from jax.experimental.pallas import tpu as pltpu
from jax.sharding import PartitionSpec as P

PULSES = 64
BEAM_TILE = 512
ELEM_TILE = 1024


def swapped(value, axis, bit):
    mask = 2**bit
    pairs = [(source, source ^ mask) for source in range(lax.axis_size(axis))]
    return lax.ppermute(value, axis, pairs)


def with_halo(block, axis, dim):
    count = lax.axis_size(axis)
    first = lax.slice_in_dim(block, 0, 1, axis=dim)
    last = lax.slice_in_dim(block, block.shape[dim] - 1, None, axis=dim)
    index = lax.axis_index(axis)
    if count == 2:
        sent = jnp.where(index == 0, last, first)
        got = lax.ppermute(sent, axis, [(0, 1), (1, 0)])
        zero = jnp.zeros_like(got)
        low = jnp.where(index == 0, zero, got)
        high = jnp.where(index == 0, got, zero)
    else:
        forward = [(i, i + 1) for i in range(count - 1)]
        backward = [(target, source) for source, target in forward]
        low = lax.ppermute(last, axis, forward)
        high = lax.ppermute(first, axis, backward)
    return jnp.concatenate([low, block, high], axis=dim)


def lag_stats(real, imag):
    zero_lag = jnp.mean(real * real + imag * imag, axis=-1)
    lag_re = jnp.sum(real[..., :-1] * real[..., 1:] + imag[..., :-1] * imag[..., 1:], axis=-1) / (
        PULSES - 1
    )
    lag_im = jnp.sum(real[..., :-1] * imag[..., 1:] - imag[..., :-1] * real[..., 1:], axis=-1) / (
        PULSES - 1
    )
    return (zero_lag, lag_re, lag_im)


def pair_stats(first, second):
    power_h = jnp.mean(first[0] * first[0] + first[1] * first[1], axis=-1)
    power_v = jnp.mean(second[0] * second[0] + second[1] * second[1], axis=-1)
    cross_re = jnp.mean(first[0] * second[0] + first[1] * second[1], axis=-1)
    cross_im = jnp.mean(first[0] * second[1] - first[1] * second[0], axis=-1)
    return (power_h, power_v, cross_re, cross_im)


def beam_stats(summed, gates):
    count = summed.shape[1]
    real = summed[0].reshape(count, gates, PULSES)
    imag = summed[1].reshape(count, gates, PULSES)
    zero_lag, lag_re, lag_im = lag_stats(real, imag)
    series = jnp.stack([real, imag])
    pol_index = lax.axis_index("pol")
    other = swapped(series, "pol", 0)
    first = jnp.where(pol_index == 0, series, other)
    second = jnp.where(pol_index == 0, other, series)
    pair = jnp.stack(pair_stats(first, second))
    return jnp.concatenate([jnp.stack([zero_lag, lag_re, lag_im]), pair], axis=0)


def complex_kernel(w_ref, x_ref, o_ref):
    bt = w_ref.shape[1]
    rows = w_ref[...].reshape(2 * bt, w_ref.shape[2])
    with_re = jnp.dot(rows, x_ref[0], preferred_element_type=jnp.float32)
    with_im = jnp.dot(rows, x_ref[1], preferred_element_type=jnp.float32)
    real = with_re[:bt] + with_im[bt:]
    imag = with_im[:bt] - with_re[bt:]

    @pl.when(pl.program_id(1) == 0)
    def _():
        o_ref[0] = real
        o_ref[1] = imag

    @pl.when(pl.program_id(1) > 0)
    def _():
        o_ref[0] += real
        o_ref[1] += imag


def partials(signal, weights):
    w = weights[:, 0]
    x = signal[:, 0]
    beams, elems = w.shape[1], w.shape[2]
    samples = x.shape[2]
    bt = min(BEAM_TILE, beams)
    tk = min(ELEM_TILE, elems)
    return pl.pallas_call(
        complex_kernel,
        out_shape=jax.ShapeDtypeStruct((2, beams, samples), jnp.float32),
        grid=(beams // bt, elems // tk),
        in_specs=[
            pl.BlockSpec((2, bt, tk), lambda i, k: (0, i, k)),
            pl.BlockSpec((2, tk, samples), lambda i, k: (0, k, 0)),
        ],
        out_specs=pl.BlockSpec((2, bt, samples), lambda i, k: (0, i, 0)),
        compiler_params=pltpu.CompilerParams(
            dimension_semantics=("arbitrary", "arbitrary"), vmem_limit_bytes=48 * 1024 * 1024
        ),
        cost_estimate=pl.CostEstimate(
            flops=8 * beams * elems * samples,
            transcendentals=0,
            bytes_accessed=4 * beams * elems + 4 * elems * samples * (beams // bt) + 8 * beams * samples,
        ),
    )(w, x)


def on_device(signal, weights):
    n_elem = lax.axis_size("elem")
    samples = signal.shape[3]
    gates = samples // PULSES
    beams = weights.shape[2]
    part = partials(signal, weights)
    summed = lax.psum_scatter(part, "elem", scatter_dimension=1, tiled=True)
    stats = beam_stats(summed, gates)
    padded = with_halo(stats, "gate", 2)
    smoothed = (padded[..., :-2] + 2.0 * padded[..., 1:-1] + padded[..., 2:]) * 0.25
    power = smoothed[0]
    magnitude = jnp.sqrt(smoothed[1] * smoothed[1] + smoothed[2] * smoothed[2])
    floor_mag = jnp.maximum(magnitude, 0.25 * power)
    moments = jnp.stack(
        [
            10.0 * jnp.log10(power + 1e-06),
            smoothed[1] / floor_mag,
            smoothed[2] / floor_mag,
            jnp.log(power / floor_mag),
        ]
    )
    zdr = 10.0 * jnp.log10((smoothed[3] + 1e-06) / (smoothed[4] + 1e-06))
    corr = jnp.sqrt(smoothed[5] * smoothed[5] + smoothed[6] * smoothed[6]) / jnp.sqrt(
        smoothed[3] * smoothed[4]
    )
    pol_index = lax.axis_index("pol")
    polar = jnp.where(pol_index == 0, zdr, corr)
    return (moments[:, None], polar[None])


def solution(mesh):
    return jax.shard_map(
        on_device,
        mesh=mesh,
        in_specs=(P("arrays", "pol", "elem", "gate"), P("arrays", "pol", None, "elem")),
        out_specs=(
            P(None, ("arrays", "pol"), "elem", "gate"),
            P("pol", ("arrays", "elem"), "gate"),
        ),
        check_vma=False,
    )
```

```python
import jax
import jax.numpy as jnp
from jax import lax
from jax.experimental import pallas as pl
from jax.experimental.pallas import tpu as pltpu
from jax.sharding import PartitionSpec as P

PULSES = 64
BEAM_TILE = 512
ELEM_TILE = 1024


def swapped(value, axis, bit):
    mask = 2**bit
    pairs = [(source, source ^ mask) for source in range(lax.axis_size(axis))]
    return lax.ppermute(value, axis, pairs)


def with_halo(block, axis, dim):
    count = lax.axis_size(axis)
    first = lax.slice_in_dim(block, 0, 1, axis=dim)
    last = lax.slice_in_dim(block, block.shape[dim] - 1, None, axis=dim)
    index = lax.axis_index(axis)
    if count == 2:
        sent = jnp.where(index == 0, last, first)
        got = lax.ppermute(sent, axis, [(0, 1), (1, 0)])
        zero = jnp.zeros_like(got)
        low = jnp.where(index == 0, zero, got)
        high = jnp.where(index == 0, got, zero)
    else:
        forward = [(i, i + 1) for i in range(count - 1)]
        backward = [(target, source) for source, target in forward]
        low = lax.ppermute(last, axis, forward)
        high = lax.ppermute(first, axis, backward)
    return jnp.concatenate([low, block, high], axis=dim)


def lag_stats(real, imag):
    zero_lag = jnp.mean(real * real + imag * imag, axis=-1)
    lag_re = jnp.sum(real[..., :-1] * real[..., 1:] + imag[..., :-1] * imag[..., 1:], axis=-1) / (
        PULSES - 1
    )
    lag_im = jnp.sum(real[..., :-1] * imag[..., 1:] - imag[..., :-1] * real[..., 1:], axis=-1) / (
        PULSES - 1
    )
    return (zero_lag, lag_re, lag_im)


def pair_stats(first, second):
    power_h = jnp.mean(first[0] * first[0] + first[1] * first[1], axis=-1)
    power_v = jnp.mean(second[0] * second[0] + second[1] * second[1], axis=-1)
    cross_re = jnp.mean(first[0] * second[0] + first[1] * second[1], axis=-1)
    cross_im = jnp.mean(first[0] * second[1] - first[1] * second[0], axis=-1)
    return (power_h, power_v, cross_re, cross_im)


def beam_stats(summed, gates):
    count = summed.shape[1]
    real = summed[0].reshape(count, gates, PULSES)
    imag = summed[1].reshape(count, gates, PULSES)
    zero_lag, lag_re, lag_im = lag_stats(real, imag)
    series = jnp.stack([real, imag])
    pol_index = lax.axis_index("pol")
    other = swapped(series, "pol", 0)
    first = jnp.where(pol_index == 0, series, other)
    second = jnp.where(pol_index == 0, other, series)
    pair = jnp.stack(pair_stats(first, second))
    return jnp.concatenate([jnp.stack([zero_lag, lag_re, lag_im]), pair], axis=0)


def complex_kernel(w_ref, x_ref, o_ref):
    bt = w_ref.shape[1]
    rows = w_ref[...].reshape(2 * bt, w_ref.shape[2])
    with_re = jnp.dot(rows, x_ref[0], preferred_element_type=jnp.float32)
    with_im = jnp.dot(rows, x_ref[1], preferred_element_type=jnp.float32)
    real = with_re[:bt] + with_im[bt:]
    imag = with_im[:bt] - with_re[bt:]

    @pl.when(pl.program_id(1) == 0)
    def _():
        o_ref[0] = real
        o_ref[1] = imag

    @pl.when(pl.program_id(1) > 0)
    def _():
        o_ref[0] += real
        o_ref[1] += imag


def partials(signal, weights):
    w = weights[:, 0]
    x = signal[:, 0]
    beams, elems = w.shape[1], w.shape[2]
    samples = x.shape[2]
    bt = min(BEAM_TILE, beams)
    tk = min(ELEM_TILE, elems)
    return pl.pallas_call(
        complex_kernel,
        out_shape=jax.ShapeDtypeStruct((2, beams, samples), jnp.float32),
        grid=(beams // bt, elems // tk),
        in_specs=[
            pl.BlockSpec((2, bt, tk), lambda i, k: (0, i, k)),
            pl.BlockSpec((2, tk, samples), lambda i, k: (0, k, 0)),
        ],
        out_specs=pl.BlockSpec((2, bt, samples), lambda i, k: (0, i, 0)),
        compiler_params=pltpu.CompilerParams(
            dimension_semantics=("arbitrary", "arbitrary"), vmem_limit_bytes=48 * 1024 * 1024
        ),
        cost_estimate=pl.CostEstimate(
            flops=8 * beams * elems * samples,
            transcendentals=0,
            bytes_accessed=4 * beams * elems + 4 * elems * samples * (beams // bt) + 8 * beams * samples,
        ),
    )(w, x)


def line_scatter(part, n_elem):
    me = lax.axis_index("elem")
    blocks = part.reshape(2, n_elem, part.shape[1] // n_elem, part.shape[2])
    got_right = None
    got_left = None
    for step in range(1, n_elem):
        to_right = lax.dynamic_index_in_dim(blocks, jnp.clip(me + n_elem - step, 0, n_elem - 1), 1, False)
        to_left = lax.dynamic_index_in_dim(blocks, jnp.clip(me - n_elem + step, 0, n_elem - 1), 1, False)
        if got_right is not None:
            to_right = to_right + got_right
            to_left = to_left + got_left
        got_right = lax.ppermute(to_right, "elem", [(c, c + 1) for c in range(step)])
        got_left = lax.ppermute(to_left, "elem", [(c, c - 1) for c in range(n_elem - step, n_elem)])
    own = lax.dynamic_index_in_dim(blocks, me, 1, False)
    if got_right is None:
        return own
    return own + got_right + got_left


def on_device(signal, weights):
    n_elem = lax.axis_size("elem")
    samples = signal.shape[3]
    gates = samples // PULSES
    beams = weights.shape[2]
    part = partials(signal, weights)
    if n_elem <= 8:
        summed = line_scatter(part, n_elem)
    else:
        summed = lax.psum_scatter(part, "elem", scatter_dimension=1, tiled=True)
    stats = beam_stats(summed, gates)
    padded = with_halo(stats, "gate", 2)
    smoothed = (padded[..., :-2] + 2.0 * padded[..., 1:-1] + padded[..., 2:]) * 0.25
    power = smoothed[0]
    magnitude = jnp.sqrt(smoothed[1] * smoothed[1] + smoothed[2] * smoothed[2])
    floor_mag = jnp.maximum(magnitude, 0.25 * power)
    moments = jnp.stack(
        [
            10.0 * jnp.log10(power + 1e-06),
            smoothed[1] / floor_mag,
            smoothed[2] / floor_mag,
            jnp.log(power / floor_mag),
        ]
    )
    zdr = 10.0 * jnp.log10((smoothed[3] + 1e-06) / (smoothed[4] + 1e-06))
    corr = jnp.sqrt(smoothed[5] * smoothed[5] + smoothed[6] * smoothed[6]) / jnp.sqrt(
        smoothed[3] * smoothed[4]
    )
    pol_index = lax.axis_index("pol")
    polar = jnp.where(pol_index == 0, zdr, corr)
    return (moments[:, None], polar[None])


def solution(mesh):
    return jax.shard_map(
        on_device,
        mesh=mesh,
        in_specs=(P("arrays", "pol", "elem", "gate"), P("arrays", "pol", None, "elem")),
        out_specs=(
            P(None, ("arrays", "pol"), "elem", "gate"),
            P("pol", ("arrays", "elem"), "gate"),
        ),
        check_vma=False,
    )
```

```python
import jax
import jax.numpy as jnp
from jax import lax
from jax.experimental import pallas as pl
from jax.experimental.pallas import tpu as pltpu
from jax.experimental.layout import Layout, with_layout_constraint
from jax.sharding import PartitionSpec as P

PULSES = 64
ROW_MAJOR = Layout(major_to_minor=(0, 1, 2))
BEAM_TILE = 512
ELEM_TILE = 1024


def swapped(value, axis, bit):
    mask = 2**bit
    pairs = [(source, source ^ mask) for source in range(lax.axis_size(axis))]
    return lax.ppermute(value, axis, pairs)


def with_halo(block, axis, dim):
    count = lax.axis_size(axis)
    first = lax.slice_in_dim(block, 0, 1, axis=dim)
    last = lax.slice_in_dim(block, block.shape[dim] - 1, None, axis=dim)
    index = lax.axis_index(axis)
    if count == 2:
        sent = jnp.where(index == 0, last, first)
        got = lax.ppermute(sent, axis, [(0, 1), (1, 0)])
        zero = jnp.zeros_like(got)
        low = jnp.where(index == 0, zero, got)
        high = jnp.where(index == 0, got, zero)
    else:
        forward = [(i, i + 1) for i in range(count - 1)]
        backward = [(target, source) for source, target in forward]
        low = lax.ppermute(last, axis, forward)
        high = lax.ppermute(first, axis, backward)
    return jnp.concatenate([low, block, high], axis=dim)


def lag_stats(real, imag):
    zero_lag = jnp.mean(real * real + imag * imag, axis=-1)
    lag_re = jnp.sum(real[..., :-1] * real[..., 1:] + imag[..., :-1] * imag[..., 1:], axis=-1) / (
        PULSES - 1
    )
    lag_im = jnp.sum(real[..., :-1] * imag[..., 1:] - imag[..., :-1] * real[..., 1:], axis=-1) / (
        PULSES - 1
    )
    return (zero_lag, lag_re, lag_im)


def pair_stats(first, second):
    power_h = jnp.mean(first[0] * first[0] + first[1] * first[1], axis=-1)
    power_v = jnp.mean(second[0] * second[0] + second[1] * second[1], axis=-1)
    cross_re = jnp.mean(first[0] * second[0] + first[1] * second[1], axis=-1)
    cross_im = jnp.mean(first[0] * second[1] - first[1] * second[0], axis=-1)
    return (power_h, power_v, cross_re, cross_im)


def beam_stats(summed, gates):
    count = summed.shape[1]
    real = summed[0].reshape(count, gates, PULSES)
    imag = summed[1].reshape(count, gates, PULSES)
    zero_lag, lag_re, lag_im = lag_stats(real, imag)
    series = jnp.stack([real, imag])
    pol_index = lax.axis_index("pol")
    other = swapped(series, "pol", 0)
    first = jnp.where(pol_index == 0, series, other)
    second = jnp.where(pol_index == 0, other, series)
    pair = jnp.stack(pair_stats(first, second))
    return jnp.concatenate([jnp.stack([zero_lag, lag_re, lag_im]), pair], axis=0)


def complex_kernel(w_ref, x_ref, o_ref):
    bt = w_ref.shape[1]
    rows = w_ref[...].reshape(2 * bt, w_ref.shape[2])
    with_re = jnp.dot(rows, x_ref[0], preferred_element_type=jnp.float32)
    with_im = jnp.dot(rows, x_ref[1], preferred_element_type=jnp.float32)
    real = with_re[:bt] + with_im[bt:]
    imag = with_im[:bt] - with_re[bt:]

    @pl.when(pl.program_id(1) == 0)
    def _():
        o_ref[0] = real
        o_ref[1] = imag

    @pl.when(pl.program_id(1) > 0)
    def _():
        o_ref[0] += real
        o_ref[1] += imag


def partials(signal, weights):
    w = weights[:, 0]
    x = signal[:, 0]
    beams, elems = w.shape[1], w.shape[2]
    samples = x.shape[2]
    bt = min(BEAM_TILE, beams)
    tk = min(ELEM_TILE, elems)
    return pl.pallas_call(
        complex_kernel,
        out_shape=jax.ShapeDtypeStruct((2, beams, samples), jnp.float32),
        grid=(beams // bt, elems // tk),
        in_specs=[
            pl.BlockSpec((2, bt, tk), lambda i, k: (0, i, k)),
            pl.BlockSpec((2, tk, samples), lambda i, k: (0, k, 0)),
        ],
        out_specs=pl.BlockSpec((2, bt, samples), lambda i, k: (0, i, 0)),
        compiler_params=pltpu.CompilerParams(
            dimension_semantics=("arbitrary", "arbitrary"), vmem_limit_bytes=48 * 1024 * 1024
        ),
        cost_estimate=pl.CostEstimate(
            flops=8 * beams * elems * samples,
            transcendentals=0,
            bytes_accessed=4 * beams * elems + 4 * elems * samples * (beams // bt) + 8 * beams * samples,
        ),
    )(w, x)


def line_scatter(part, n_elem):
    me = lax.axis_index("elem")
    blocks = part.reshape(2, n_elem, part.shape[1] // n_elem, part.shape[2])
    got_right = None
    got_left = None
    for step in range(1, n_elem):
        to_right = lax.dynamic_index_in_dim(blocks, jnp.clip(me + n_elem - step, 0, n_elem - 1), 1, False)
        to_left = lax.dynamic_index_in_dim(blocks, jnp.clip(me - n_elem + step, 0, n_elem - 1), 1, False)
        if got_right is not None:
            to_right = to_right + got_right
            to_left = to_left + got_left
        to_right = with_layout_constraint(to_right, ROW_MAJOR)
        to_left = with_layout_constraint(to_left, ROW_MAJOR)
        got_right = lax.ppermute(to_right, "elem", [(c, c + 1) for c in range(step)])
        got_left = lax.ppermute(to_left, "elem", [(c, c - 1) for c in range(n_elem - step, n_elem)])
    own = lax.dynamic_index_in_dim(blocks, me, 1, False)
    if got_right is None:
        return own
    return own + got_right + got_left


def on_device(signal, weights):
    n_elem = lax.axis_size("elem")
    samples = signal.shape[3]
    gates = samples // PULSES
    beams = weights.shape[2]
    part = partials(signal, weights)
    if n_elem <= 8:
        summed = line_scatter(part, n_elem)
    else:
        summed = lax.psum_scatter(part, "elem", scatter_dimension=1, tiled=True)
    stats = beam_stats(summed, gates)
    padded = with_halo(stats, "gate", 2)
    smoothed = (padded[..., :-2] + 2.0 * padded[..., 1:-1] + padded[..., 2:]) * 0.25
    power = smoothed[0]
    magnitude = jnp.sqrt(smoothed[1] * smoothed[1] + smoothed[2] * smoothed[2])
    floor_mag = jnp.maximum(magnitude, 0.25 * power)
    moments = jnp.stack(
        [
            10.0 * jnp.log10(power + 1e-06),
            smoothed[1] / floor_mag,
            smoothed[2] / floor_mag,
            jnp.log(power / floor_mag),
        ]
    )
    zdr = 10.0 * jnp.log10((smoothed[3] + 1e-06) / (smoothed[4] + 1e-06))
    corr = jnp.sqrt(smoothed[5] * smoothed[5] + smoothed[6] * smoothed[6]) / jnp.sqrt(
        smoothed[3] * smoothed[4]
    )
    pol_index = lax.axis_index("pol")
    polar = jnp.where(pol_index == 0, zdr, corr)
    return (moments[:, None], polar[None])


def solution(mesh):
    return jax.shard_map(
        on_device,
        mesh=mesh,
        in_specs=(P("arrays", "pol", "elem", "gate"), P("arrays", "pol", None, "elem")),
        out_specs=(
            P(None, ("arrays", "pol"), "elem", "gate"),
            P("pol", ("arrays", "elem"), "gate"),
        ),
        check_vma=False,
    )
```

```python
import jax
import jax.numpy as jnp
from jax import lax
from jax.experimental import pallas as pl
from jax.experimental.pallas import tpu as pltpu
from jax.sharding import PartitionSpec as P

PULSES = 64
BEAM_TILE = 512
ELEM_TILE = 1024


def swapped(value, axis, bit):
    mask = 2**bit
    pairs = [(source, source ^ mask) for source in range(lax.axis_size(axis))]
    return lax.ppermute(value, axis, pairs)


def with_halo(block, axis, dim):
    count = lax.axis_size(axis)
    first = lax.slice_in_dim(block, 0, 1, axis=dim)
    last = lax.slice_in_dim(block, block.shape[dim] - 1, None, axis=dim)
    index = lax.axis_index(axis)
    if count == 2:
        sent = jnp.where(index == 0, last, first)
        got = lax.ppermute(sent, axis, [(0, 1), (1, 0)])
        zero = jnp.zeros_like(got)
        low = jnp.where(index == 0, zero, got)
        high = jnp.where(index == 0, got, zero)
    else:
        forward = [(i, i + 1) for i in range(count - 1)]
        backward = [(target, source) for source, target in forward]
        low = lax.ppermute(last, axis, forward)
        high = lax.ppermute(first, axis, backward)
    return jnp.concatenate([low, block, high], axis=dim)


def lag_stats(real, imag):
    zero_lag = jnp.mean(real * real + imag * imag, axis=-1)
    lag_re = jnp.sum(real[..., :-1] * real[..., 1:] + imag[..., :-1] * imag[..., 1:], axis=-1) / (
        PULSES - 1
    )
    lag_im = jnp.sum(real[..., :-1] * imag[..., 1:] - imag[..., :-1] * real[..., 1:], axis=-1) / (
        PULSES - 1
    )
    return (zero_lag, lag_re, lag_im)


def pair_stats(first, second):
    power_h = jnp.mean(first[0] * first[0] + first[1] * first[1], axis=-1)
    power_v = jnp.mean(second[0] * second[0] + second[1] * second[1], axis=-1)
    cross_re = jnp.mean(first[0] * second[0] + first[1] * second[1], axis=-1)
    cross_im = jnp.mean(first[0] * second[1] - first[1] * second[0], axis=-1)
    return (power_h, power_v, cross_re, cross_im)


def beam_stats(summed, gates):
    count = summed.shape[1]
    real = summed[0].reshape(count, gates, PULSES)
    imag = summed[1].reshape(count, gates, PULSES)
    zero_lag, lag_re, lag_im = lag_stats(real, imag)
    series = jnp.stack([real, imag])
    pol_index = lax.axis_index("pol")
    other = swapped(series, "pol", 0)
    first = jnp.where(pol_index == 0, series, other)
    second = jnp.where(pol_index == 0, other, series)
    pair = jnp.stack(pair_stats(first, second))
    return jnp.concatenate([jnp.stack([zero_lag, lag_re, lag_im]), pair], axis=0)


def complex_kernel(half_ref, w_ref, x_ref, o_ref):
    bt = w_ref.shape[1]
    rows = w_ref[...].reshape(2 * bt, w_ref.shape[2])
    with_re = jnp.dot(rows, x_ref[0], preferred_element_type=jnp.float32)
    with_im = jnp.dot(rows, x_ref[1], preferred_element_type=jnp.float32)
    real = with_re[:bt] + with_im[bt:]
    imag = with_im[:bt] - with_re[bt:]

    @pl.when(pl.program_id(1) == 0)
    def _():
        o_ref[0] = real
        o_ref[1] = imag

    @pl.when(pl.program_id(1) > 0)
    def _():
        o_ref[0] += real
        o_ref[1] += imag


def partials(signal, weights, half=None):
    w = weights[:, 0]
    x = signal[:, 0]
    beams, elems = w.shape[1], w.shape[2]
    samples = x.shape[2]
    rows = beams if half is None else beams // 2
    bt = min(BEAM_TILE, rows)
    tk = min(ELEM_TILE, elems)
    tiles = rows // bt
    if half is None:
        half = jnp.zeros((1,), jnp.int32)
    return pl.pallas_call(
        complex_kernel,
        out_shape=jax.ShapeDtypeStruct((2, rows, samples), jnp.float32),
        grid_spec=pltpu.PrefetchScalarGridSpec(
            num_scalar_prefetch=1,
            grid=(tiles, elems // tk),
            in_specs=[
                pl.BlockSpec((2, bt, tk), lambda i, k, h: (0, h[0] * tiles + i, k)),
                pl.BlockSpec((2, tk, samples), lambda i, k, h: (0, k, 0)),
            ],
            out_specs=pl.BlockSpec((2, bt, samples), lambda i, k, h: (0, i, 0)),
        ),
        compiler_params=pltpu.CompilerParams(
            dimension_semantics=("arbitrary", "arbitrary"), vmem_limit_bytes=48 * 1024 * 1024
        ),
        cost_estimate=pl.CostEstimate(
            flops=8 * rows * elems * samples,
            transcendentals=0,
            bytes_accessed=4 * rows * elems + 4 * elems * samples * tiles + 8 * rows * samples,
        ),
    )(half, w, x)


def line_scatter(signal, weights, n_elem):
    me = lax.axis_index("elem")
    lower = me >= n_elem // 2
    first_base = jnp.where(lower, 0, n_elem // 2)
    second_base = n_elem // 2 - first_base
    first = partials(signal, weights, (1 - lower.astype(jnp.int32)).reshape(1))
    second = partials(signal, weights, lower.astype(jnp.int32).reshape(1))
    count = n_elem // 2
    first = first.reshape(2, count, first.shape[1] // count, first.shape[2])
    second = second.reshape(2, count, second.shape[1] // count, second.shape[2])

    def block(q, late):
        from_first = lax.dynamic_index_in_dim(first, jnp.clip(q - first_base, 0, count - 1), 1, False)
        if not late:
            return from_first
        from_second = lax.dynamic_index_in_dim(second, jnp.clip(q - second_base, 0, count - 1), 1, False)
        in_first = (q >= first_base) & (q < first_base + count)
        return jnp.where(in_first, from_first, from_second)

    got_right = None
    got_left = None
    for step in range(1, n_elem):
        late = step > n_elem // 2
        to_right = block(me + n_elem - step, late)
        to_left = block(me - n_elem + step, late)
        if got_right is not None:
            to_right = to_right + got_right
            to_left = to_left + got_left
        got_right = lax.ppermute(to_right, "elem", [(c, c + 1) for c in range(step)])
        got_left = lax.ppermute(to_left, "elem", [(c, c - 1) for c in range(n_elem - step, n_elem)])
    own = lax.dynamic_index_in_dim(second, jnp.clip(me - second_base, 0, count - 1), 1, False)
    return own + got_right + got_left


def on_device(signal, weights):
    n_elem = lax.axis_size("elem")
    samples = signal.shape[3]
    gates = samples // PULSES
    beams = weights.shape[2]
    if 2 <= n_elem <= 8 and n_elem % 2 == 0:
        summed = line_scatter(signal, weights, n_elem)
    else:
        part = partials(signal, weights)
        summed = lax.psum_scatter(part, "elem", scatter_dimension=1, tiled=True)
    stats = beam_stats(summed, gates)
    padded = with_halo(stats, "gate", 2)
    smoothed = (padded[..., :-2] + 2.0 * padded[..., 1:-1] + padded[..., 2:]) * 0.25
    power = smoothed[0]
    magnitude = jnp.sqrt(smoothed[1] * smoothed[1] + smoothed[2] * smoothed[2])
    floor_mag = jnp.maximum(magnitude, 0.25 * power)
    moments = jnp.stack(
        [
            10.0 * jnp.log10(power + 1e-06),
            smoothed[1] / floor_mag,
            smoothed[2] / floor_mag,
            jnp.log(power / floor_mag),
        ]
    )
    zdr = 10.0 * jnp.log10((smoothed[3] + 1e-06) / (smoothed[4] + 1e-06))
    corr = jnp.sqrt(smoothed[5] * smoothed[5] + smoothed[6] * smoothed[6]) / jnp.sqrt(
        smoothed[3] * smoothed[4]
    )
    pol_index = lax.axis_index("pol")
    polar = jnp.where(pol_index == 0, zdr, corr)
    return (moments[:, None], polar[None])


def solution(mesh):
    return jax.shard_map(
        on_device,
        mesh=mesh,
        in_specs=(P("arrays", "pol", "elem", "gate"), P("arrays", "pol", None, "elem")),
        out_specs=(
            P(None, ("arrays", "pol"), "elem", "gate"),
            P("pol", ("arrays", "elem"), "gate"),
        ),
        check_vma=False,
    )
```

```python
import jax
import jax.numpy as jnp
from jax import lax
from jax.experimental import pallas as pl
from jax.experimental.pallas import tpu as pltpu
from jax.sharding import PartitionSpec as P

PULSES = 64
BEAM_TILE = 512
ELEM_TILE = 1024


def swapped(value, axis, bit):
    mask = 2**bit
    pairs = [(source, source ^ mask) for source in range(lax.axis_size(axis))]
    return lax.ppermute(value, axis, pairs)


def with_halo(block, axis, dim):
    count = lax.axis_size(axis)
    first = lax.slice_in_dim(block, 0, 1, axis=dim)
    last = lax.slice_in_dim(block, block.shape[dim] - 1, None, axis=dim)
    index = lax.axis_index(axis)
    if count == 2:
        sent = jnp.where(index == 0, last, first)
        got = lax.ppermute(sent, axis, [(0, 1), (1, 0)])
        zero = jnp.zeros_like(got)
        low = jnp.where(index == 0, zero, got)
        high = jnp.where(index == 0, got, zero)
    else:
        forward = [(i, i + 1) for i in range(count - 1)]
        backward = [(target, source) for source, target in forward]
        low = lax.ppermute(last, axis, forward)
        high = lax.ppermute(first, axis, backward)
    return jnp.concatenate([low, block, high], axis=dim)


def lag_stats(real, imag):
    zero_lag = jnp.mean(real * real + imag * imag, axis=-1)
    lag_re = jnp.sum(real[..., :-1] * real[..., 1:] + imag[..., :-1] * imag[..., 1:], axis=-1) / (
        PULSES - 1
    )
    lag_im = jnp.sum(real[..., :-1] * imag[..., 1:] - imag[..., :-1] * real[..., 1:], axis=-1) / (
        PULSES - 1
    )
    return (zero_lag, lag_re, lag_im)


def pair_stats(first, second):
    power_h = jnp.mean(first[0] * first[0] + first[1] * first[1], axis=-1)
    power_v = jnp.mean(second[0] * second[0] + second[1] * second[1], axis=-1)
    cross_re = jnp.mean(first[0] * second[0] + first[1] * second[1], axis=-1)
    cross_im = jnp.mean(first[0] * second[1] - first[1] * second[0], axis=-1)
    return (power_h, power_v, cross_re, cross_im)


def beam_stats(summed, gates):
    count = summed.shape[1]
    real = summed[0].reshape(count, gates, PULSES)
    imag = summed[1].reshape(count, gates, PULSES)
    zero_lag, lag_re, lag_im = lag_stats(real, imag)
    series = jnp.stack([real, imag])
    pol_index = lax.axis_index("pol")
    other = swapped(series, "pol", 0)
    first = jnp.where(pol_index == 0, series, other)
    second = jnp.where(pol_index == 0, other, series)
    pair = jnp.stack(pair_stats(first, second))
    return jnp.concatenate([jnp.stack([zero_lag, lag_re, lag_im]), pair], axis=0)


def complex_kernel(half_ref, w_ref, x_ref, o_ref):
    bt = w_ref.shape[1]
    rows = w_ref[...].reshape(2 * bt, w_ref.shape[2])
    with_re = jnp.dot(rows, x_ref[0], preferred_element_type=jnp.float32)
    with_im = jnp.dot(rows, x_ref[1], preferred_element_type=jnp.float32)
    real = with_re[:bt] + with_im[bt:]
    imag = with_im[:bt] - with_re[bt:]

    @pl.when(pl.program_id(1) == 0)
    def _():
        o_ref[0] = real
        o_ref[1] = imag

    @pl.when(pl.program_id(1) > 0)
    def _():
        o_ref[0] += real
        o_ref[1] += imag


def partials(signal, weights, half=None):
    w = weights[:, 0]
    x = signal[:, 0]
    beams, elems = w.shape[1], w.shape[2]
    samples = x.shape[2]
    rows = beams if half is None else beams // 2
    bt = min(BEAM_TILE, rows)
    tk = min(ELEM_TILE, elems)
    tiles = rows // bt
    if half is None:
        half = jnp.zeros((1,), jnp.int32)
    return pl.pallas_call(
        complex_kernel,
        out_shape=jax.ShapeDtypeStruct((2, rows, samples), jnp.float32),
        grid_spec=pltpu.PrefetchScalarGridSpec(
            num_scalar_prefetch=1,
            grid=(tiles, elems // tk),
            in_specs=[
                pl.BlockSpec((2, bt, tk), lambda i, k, h: (0, h[0] * tiles + i, k)),
                pl.BlockSpec((2, tk, samples), lambda i, k, h: (0, k, 0)),
            ],
            out_specs=pl.BlockSpec((2, bt, samples), lambda i, k, h: (0, i, 0)),
        ),
        compiler_params=pltpu.CompilerParams(
            dimension_semantics=("arbitrary", "arbitrary"), vmem_limit_bytes=48 * 1024 * 1024
        ),
        cost_estimate=pl.CostEstimate(
            flops=8 * rows * elems * samples,
            transcendentals=0,
            bytes_accessed=4 * rows * elems + 4 * elems * samples * tiles + 8 * rows * samples,
        ),
    )(half, w, x)


def block_kernel(index_ref, w_ref, x_ref, o_ref, acc_ref):
    bt = w_ref.shape[1]
    rows = w_ref[...].reshape(2 * bt, w_ref.shape[2])
    with_re = jnp.dot(rows, x_ref[0], preferred_element_type=jnp.float32)
    with_im = jnp.dot(rows, x_ref[1], preferred_element_type=jnp.float32)
    real = with_re[:bt] + with_im[bt:]
    imag = with_im[:bt] - with_re[bt:]
    step = pl.program_id(0)

    @pl.when(step == 0)
    def _():
        acc_ref[0] = real
        acc_ref[1] = imag

    @pl.when(step > 0)
    def _():
        acc_ref[0] += real
        acc_ref[1] += imag

    @pl.when(step == pl.num_programs(0) - 1)
    def _():
        o_ref[0] = acc_ref[0].T
        o_ref[1] = acc_ref[1].T


def block_partial(signal, weights, index, count):
    w = weights[:, 0]
    x = signal[:, 0]
    elems = w.shape[2]
    samples = x.shape[2]
    tk = min(ELEM_TILE, elems)
    return pl.pallas_call(
        block_kernel,
        out_shape=jax.ShapeDtypeStruct((2, samples, count), jnp.float32),
        grid_spec=pltpu.PrefetchScalarGridSpec(
            num_scalar_prefetch=1,
            grid=(elems // tk,),
            in_specs=[
                pl.BlockSpec((2, count, tk), lambda k, b: (0, b[0], k)),
                pl.BlockSpec((2, tk, samples), lambda k, b: (0, k, 0)),
            ],
            out_specs=pl.BlockSpec((2, samples, count), lambda k, b: (0, 0, 0)),
            scratch_shapes=[pltpu.VMEM((2, count, samples), jnp.float32)],
        ),
        compiler_params=pltpu.CompilerParams(
            dimension_semantics=("arbitrary",), vmem_limit_bytes=48 * 1024 * 1024
        ),
        cost_estimate=pl.CostEstimate(
            flops=8 * count * elems * samples,
            transcendentals=0,
            bytes_accessed=4 * count * elems + 4 * elems * samples + 8 * count * samples,
        ),
    )(index.reshape(1), w, x)


def line_scatter(signal, weights, n_elem):
    me = lax.axis_index("elem")
    near = me < n_elem // 2
    local = weights.shape[2] // n_elem

    def order(c, q):
        return n_elem - 1 - q if c < n_elem // 2 else q

    made = []
    for k in range(n_elem):
        index = jnp.where(near, n_elem - 1 - k, k).astype(jnp.int32)
        made.append(jnp.swapaxes(block_partial(signal, weights, index, local), 1, 2))

    def pick(q, needed):
        at = jnp.where(near, n_elem - 1 - q, q)
        picked = made[needed[0]]
        for k in needed[1:]:
            picked = jnp.where(at == k, made[k], picked)
        return picked

    got_right = None
    got_left = None
    for step in range(1, n_elem):
        senders_right = range(step)
        senders_left = range(n_elem - step, n_elem)
        need_right = sorted({order(c, c + n_elem - step) for c in senders_right})
        need_left = sorted({order(c, c - n_elem + step) for c in senders_left})
        to_right = pick(me + n_elem - step, need_right)
        to_left = pick(me - n_elem + step, need_left)
        if got_right is not None:
            to_right = to_right + got_right
            to_left = to_left + got_left
        got_right = lax.ppermute(to_right, "elem", [(c, c + 1) for c in senders_right])
        got_left = lax.ppermute(to_left, "elem", [(c, c - 1) for c in senders_left])
    own = pick(me, sorted({order(c, c) for c in range(n_elem)}))
    return own + got_right + got_left


def on_device(signal, weights):
    n_elem = lax.axis_size("elem")
    samples = signal.shape[3]
    gates = samples // PULSES
    beams = weights.shape[2]
    if 2 <= n_elem <= 8 and n_elem % 2 == 0:
        summed = line_scatter(signal, weights, n_elem)
    else:
        part = partials(signal, weights)
        summed = lax.psum_scatter(part, "elem", scatter_dimension=1, tiled=True)
    stats = beam_stats(summed, gates)
    padded = with_halo(stats, "gate", 2)
    smoothed = (padded[..., :-2] + 2.0 * padded[..., 1:-1] + padded[..., 2:]) * 0.25
    power = smoothed[0]
    magnitude = jnp.sqrt(smoothed[1] * smoothed[1] + smoothed[2] * smoothed[2])
    floor_mag = jnp.maximum(magnitude, 0.25 * power)
    moments = jnp.stack(
        [
            10.0 * jnp.log10(power + 1e-06),
            smoothed[1] / floor_mag,
            smoothed[2] / floor_mag,
            jnp.log(power / floor_mag),
        ]
    )
    zdr = 10.0 * jnp.log10((smoothed[3] + 1e-06) / (smoothed[4] + 1e-06))
    corr = jnp.sqrt(smoothed[5] * smoothed[5] + smoothed[6] * smoothed[6]) / jnp.sqrt(
        smoothed[3] * smoothed[4]
    )
    pol_index = lax.axis_index("pol")
    polar = jnp.where(pol_index == 0, zdr, corr)
    return (moments[:, None], polar[None])


def solution(mesh):
    return jax.shard_map(
        on_device,
        mesh=mesh,
        in_specs=(P("arrays", "pol", "elem", "gate"), P("arrays", "pol", None, "elem")),
        out_specs=(
            P(None, ("arrays", "pol"), "elem", "gate"),
            P("pol", ("arrays", "elem"), "gate"),
        ),
        check_vma=False,
    )
```

```python
import jax
import jax.numpy as jnp
from jax import lax
from jax.experimental import pallas as pl
from jax.experimental.pallas import tpu as pltpu
from jax.sharding import PartitionSpec as P

PULSES = 64
BEAM_TILE = 512
ELEM_TILE = 1024


def swapped(value, axis, bit):
    mask = 2**bit
    pairs = [(source, source ^ mask) for source in range(lax.axis_size(axis))]
    return lax.ppermute(value, axis, pairs)


def lag_stats(real, imag):
    zero_lag = jnp.mean(real * real + imag * imag, axis=-1)
    lag_re = jnp.sum(real[..., :-1] * real[..., 1:] + imag[..., :-1] * imag[..., 1:], axis=-1) / (
        PULSES - 1
    )
    lag_im = jnp.sum(real[..., :-1] * imag[..., 1:] - imag[..., :-1] * real[..., 1:], axis=-1) / (
        PULSES - 1
    )
    return (zero_lag, lag_re, lag_im)


def pair_stats(first, second):
    power_h = jnp.mean(first[0] * first[0] + first[1] * first[1], axis=-1)
    power_v = jnp.mean(second[0] * second[0] + second[1] * second[1], axis=-1)
    cross_re = jnp.mean(first[0] * second[0] + first[1] * second[1], axis=-1)
    cross_im = jnp.mean(first[0] * second[1] - first[1] * second[0], axis=-1)
    return (power_h, power_v, cross_re, cross_im)


def beam_stats(summed, gates):
    count = summed.shape[1]
    series = summed.reshape(2, count, gates, PULSES)
    pol_index = lax.axis_index("pol")
    other = swapped(series, "pol", 0)
    n_gate = lax.axis_size("gate")
    n_pol = lax.axis_size("pol")
    gate_index = lax.axis_index("gate")
    first = series[:, :, :1]
    last = series[:, :, gates - 1 :]
    both = ("gate", "pol")

    def across(g, p):
        return g * n_pol + (n_pol - 1 - p)

    if n_gate == 2:
        sent = jnp.where(gate_index == 0, last, first)
        got_own = lax.ppermute(sent, "gate", [(0, 1), (1, 0)])
        got_other = lax.ppermute(sent, both, [(g * n_pol + p, across(1 - g, p)) for g in range(2) for p in range(n_pol)])
        zero = jnp.zeros_like(got_own)
        low_own = jnp.where(gate_index == 0, zero, got_own)
        high_own = jnp.where(gate_index == 0, got_own, zero)
        low_other = jnp.where(gate_index == 0, zero, got_other)
        high_other = jnp.where(gate_index == 0, got_other, zero)
    else:
        forward = [(i, i + 1) for i in range(n_gate - 1)]
        backward = [(i + 1, i) for i in range(n_gate - 1)]
        low_own = lax.ppermute(last, "gate", forward)
        high_own = lax.ppermute(first, "gate", backward)
        low_other = lax.ppermute(
            last, both, [(g * n_pol + p, across(g + 1, p)) for g in range(n_gate - 1) for p in range(n_pol)]
        )
        high_other = lax.ppermute(
            first, both, [((g + 1) * n_pol + p, across(g, p)) for g in range(n_gate - 1) for p in range(n_pol)]
        )
    own = jnp.concatenate([low_own, series, high_own], axis=2)
    partner = jnp.concatenate([low_other, other, high_other], axis=2)
    zero_lag, lag_re, lag_im = lag_stats(own[0], own[1])
    first_pol = jnp.where(pol_index == 0, own, partner)
    second_pol = jnp.where(pol_index == 0, partner, own)
    pair = jnp.stack(pair_stats(first_pol, second_pol))
    return jnp.concatenate([jnp.stack([zero_lag, lag_re, lag_im]), pair], axis=0)


def complex_kernel(half_ref, w_ref, x_ref, o_ref):
    bt = w_ref.shape[1]
    rows = w_ref[...].reshape(2 * bt, w_ref.shape[2])
    with_re = jnp.dot(rows, x_ref[0], preferred_element_type=jnp.float32)
    with_im = jnp.dot(rows, x_ref[1], preferred_element_type=jnp.float32)
    real = with_re[:bt] + with_im[bt:]
    imag = with_im[:bt] - with_re[bt:]

    @pl.when(pl.program_id(1) == 0)
    def _():
        o_ref[0] = real
        o_ref[1] = imag

    @pl.when(pl.program_id(1) > 0)
    def _():
        o_ref[0] += real
        o_ref[1] += imag


def partials(signal, weights, half=None):
    w = weights[:, 0]
    x = signal[:, 0]
    beams, elems = w.shape[1], w.shape[2]
    samples = x.shape[2]
    rows = beams if half is None else beams // 2
    bt = min(BEAM_TILE, rows)
    tk = min(ELEM_TILE, elems)
    tiles = rows // bt
    if half is None:
        half = jnp.zeros((1,), jnp.int32)
    return pl.pallas_call(
        complex_kernel,
        out_shape=jax.ShapeDtypeStruct((2, rows, samples), jnp.float32),
        grid_spec=pltpu.PrefetchScalarGridSpec(
            num_scalar_prefetch=1,
            grid=(tiles, elems // tk),
            in_specs=[
                pl.BlockSpec((2, bt, tk), lambda i, k, h: (0, h[0] * tiles + i, k)),
                pl.BlockSpec((2, tk, samples), lambda i, k, h: (0, k, 0)),
            ],
            out_specs=pl.BlockSpec((2, bt, samples), lambda i, k, h: (0, i, 0)),
        ),
        compiler_params=pltpu.CompilerParams(
            dimension_semantics=("arbitrary", "arbitrary"), vmem_limit_bytes=48 * 1024 * 1024
        ),
        cost_estimate=pl.CostEstimate(
            flops=8 * rows * elems * samples,
            transcendentals=0,
            bytes_accessed=4 * rows * elems + 4 * elems * samples * tiles + 8 * rows * samples,
        ),
    )(half, w, x)


def block_kernel(index_ref, w_ref, x_ref, o_ref, acc_ref):
    bt = w_ref.shape[1]
    rows = w_ref[...].reshape(2 * bt, w_ref.shape[2])
    with_re = jnp.dot(rows, x_ref[0], preferred_element_type=jnp.float32)
    with_im = jnp.dot(rows, x_ref[1], preferred_element_type=jnp.float32)
    real = with_re[:bt] + with_im[bt:]
    imag = with_im[:bt] - with_re[bt:]
    step = pl.program_id(0)

    @pl.when(step == 0)
    def _():
        acc_ref[0] = real
        acc_ref[1] = imag

    @pl.when(step > 0)
    def _():
        acc_ref[0] += real
        acc_ref[1] += imag

    @pl.when(step == pl.num_programs(0) - 1)
    def _():
        o_ref[0] = acc_ref[0].T
        o_ref[1] = acc_ref[1].T


def block_partial(signal, weights, index, count):
    w = weights[:, 0]
    x = signal[:, 0]
    elems = w.shape[2]
    samples = x.shape[2]
    tk = min(ELEM_TILE, elems)
    return pl.pallas_call(
        block_kernel,
        out_shape=jax.ShapeDtypeStruct((2, samples, count), jnp.float32),
        grid_spec=pltpu.PrefetchScalarGridSpec(
            num_scalar_prefetch=1,
            grid=(elems // tk,),
            in_specs=[
                pl.BlockSpec((2, count, tk), lambda k, b: (0, b[0], k)),
                pl.BlockSpec((2, tk, samples), lambda k, b: (0, k, 0)),
            ],
            out_specs=pl.BlockSpec((2, samples, count), lambda k, b: (0, 0, 0)),
            scratch_shapes=[pltpu.VMEM((2, count, samples), jnp.float32)],
        ),
        compiler_params=pltpu.CompilerParams(
            dimension_semantics=("arbitrary",), vmem_limit_bytes=48 * 1024 * 1024
        ),
        cost_estimate=pl.CostEstimate(
            flops=8 * count * elems * samples,
            transcendentals=0,
            bytes_accessed=4 * count * elems + 4 * elems * samples + 8 * count * samples,
        ),
    )(index.reshape(1), w, x)


def line_scatter(signal, weights, n_elem):
    me = lax.axis_index("elem")
    near = me < n_elem // 2
    local = weights.shape[2] // n_elem

    def order(c, q):
        return n_elem - 1 - q if c < n_elem // 2 else q

    made = []
    for k in range(n_elem):
        index = jnp.where(near, n_elem - 1 - k, k).astype(jnp.int32)
        made.append(jnp.swapaxes(block_partial(signal, weights, index, local), 1, 2))

    def pick(q, needed):
        at = jnp.where(near, n_elem - 1 - q, q)
        picked = made[needed[0]]
        for k in needed[1:]:
            picked = jnp.where(at == k, made[k], picked)
        return picked

    got_right = None
    got_left = None
    for step in range(1, n_elem):
        senders_right = range(step)
        senders_left = range(n_elem - step, n_elem)
        need_right = sorted({order(c, c + n_elem - step) for c in senders_right})
        need_left = sorted({order(c, c - n_elem + step) for c in senders_left})
        to_right = pick(me + n_elem - step, need_right)
        to_left = pick(me - n_elem + step, need_left)
        if got_right is not None:
            to_right = to_right + got_right
            to_left = to_left + got_left
        got_right = lax.ppermute(to_right, "elem", [(c, c + 1) for c in senders_right])
        got_left = lax.ppermute(to_left, "elem", [(c, c - 1) for c in senders_left])
    own = pick(me, sorted({order(c, c) for c in range(n_elem)}))
    return own + got_right + got_left


def on_device(signal, weights):
    n_elem = lax.axis_size("elem")
    samples = signal.shape[3]
    gates = samples // PULSES
    beams = weights.shape[2]
    if 2 <= n_elem <= 8 and n_elem % 2 == 0:
        summed = line_scatter(signal, weights, n_elem)
    else:
        part = partials(signal, weights)
        summed = lax.psum_scatter(part, "elem", scatter_dimension=1, tiled=True)
    stats = beam_stats(summed, gates)
    padded = stats
    smoothed = (padded[..., :-2] + 2.0 * padded[..., 1:-1] + padded[..., 2:]) * 0.25
    power = smoothed[0]
    magnitude = jnp.sqrt(smoothed[1] * smoothed[1] + smoothed[2] * smoothed[2])
    floor_mag = jnp.maximum(magnitude, 0.25 * power)
    moments = jnp.stack(
        [
            10.0 * jnp.log10(power + 1e-06),
            smoothed[1] / floor_mag,
            smoothed[2] / floor_mag,
            jnp.log(power / floor_mag),
        ]
    )
    zdr = 10.0 * jnp.log10((smoothed[3] + 1e-06) / (smoothed[4] + 1e-06))
    corr = jnp.sqrt(smoothed[5] * smoothed[5] + smoothed[6] * smoothed[6]) / jnp.sqrt(
        smoothed[3] * smoothed[4]
    )
    pol_index = lax.axis_index("pol")
    polar = jnp.where(pol_index == 0, zdr, corr)
    return (moments[:, None], polar[None])


def solution(mesh):
    return jax.shard_map(
        on_device,
        mesh=mesh,
        in_specs=(P("arrays", "pol", "elem", "gate"), P("arrays", "pol", None, "elem")),
        out_specs=(
            P(None, ("arrays", "pol"), "elem", "gate"),
            P("pol", ("arrays", "elem"), "gate"),
        ),
        check_vma=False,
    )
```

```python
import jax
import jax.numpy as jnp
from jax import lax
from jax.experimental import pallas as pl
from jax.experimental.pallas import tpu as pltpu
from jax.sharding import PartitionSpec as P

PULSES = 64
BEAM_TILE = 512
ELEM_TILE = 1024


def swapped(value, axis, bit):
    mask = 2**bit
    pairs = [(source, source ^ mask) for source in range(lax.axis_size(axis))]
    return lax.ppermute(value, axis, pairs)


def with_halo(block, axis, dim):
    count = lax.axis_size(axis)
    first = lax.slice_in_dim(block, 0, 1, axis=dim)
    last = lax.slice_in_dim(block, block.shape[dim] - 1, None, axis=dim)
    index = lax.axis_index(axis)
    if count == 2:
        sent = jnp.where(index == 0, last, first)
        got = lax.ppermute(sent, axis, [(0, 1), (1, 0)])
        zero = jnp.zeros_like(got)
        low = jnp.where(index == 0, zero, got)
        high = jnp.where(index == 0, got, zero)
    else:
        forward = [(i, i + 1) for i in range(count - 1)]
        backward = [(target, source) for source, target in forward]
        low = lax.ppermute(last, axis, forward)
        high = lax.ppermute(first, axis, backward)
    return jnp.concatenate([low, block, high], axis=dim)


def lag_stats(real, imag):
    zero_lag = jnp.mean(real * real + imag * imag, axis=-1)
    lag_re = jnp.sum(real[..., :-1] * real[..., 1:] + imag[..., :-1] * imag[..., 1:], axis=-1) / (
        PULSES - 1
    )
    lag_im = jnp.sum(real[..., :-1] * imag[..., 1:] - imag[..., :-1] * real[..., 1:], axis=-1) / (
        PULSES - 1
    )
    return (zero_lag, lag_re, lag_im)


def pair_stats(first, second):
    power_h = jnp.mean(first[0] * first[0] + first[1] * first[1], axis=-1)
    power_v = jnp.mean(second[0] * second[0] + second[1] * second[1], axis=-1)
    cross_re = jnp.mean(first[0] * second[0] + first[1] * second[1], axis=-1)
    cross_im = jnp.mean(first[0] * second[1] - first[1] * second[0], axis=-1)
    return (power_h, power_v, cross_re, cross_im)


def beam_stats(summed, gates):
    count = summed.shape[1]
    real = summed[0].reshape(count, gates, PULSES)
    imag = summed[1].reshape(count, gates, PULSES)
    zero_lag, lag_re, lag_im = lag_stats(real, imag)
    series = jnp.stack([real, imag])
    pol_index = lax.axis_index("pol")
    other = swapped(series, "pol", 0)
    first = jnp.where(pol_index == 0, series, other)
    second = jnp.where(pol_index == 0, other, series)
    pair = jnp.stack(pair_stats(first, second))
    return jnp.concatenate([jnp.stack([zero_lag, lag_re, lag_im]), pair], axis=0)


def complex_kernel(half_ref, w_ref, x_ref, o_ref):
    bt = w_ref.shape[1]
    rows = w_ref[...].reshape(2 * bt, w_ref.shape[2])
    with_re = jnp.dot(rows, x_ref[0], preferred_element_type=jnp.float32)
    with_im = jnp.dot(rows, x_ref[1], preferred_element_type=jnp.float32)
    real = with_re[:bt] + with_im[bt:]
    imag = with_im[:bt] - with_re[bt:]

    @pl.when(pl.program_id(1) == 0)
    def _():
        o_ref[0] = real
        o_ref[1] = imag

    @pl.when(pl.program_id(1) > 0)
    def _():
        o_ref[0] += real
        o_ref[1] += imag


def partials(signal, weights, half=None):
    w = weights[:, 0]
    x = signal[:, 0]
    beams, elems = w.shape[1], w.shape[2]
    samples = x.shape[2]
    rows = beams if half is None else beams // 2
    bt = min(BEAM_TILE, rows)
    tk = min(ELEM_TILE, elems)
    tiles = rows // bt
    if half is None:
        half = jnp.zeros((1,), jnp.int32)
    return pl.pallas_call(
        complex_kernel,
        out_shape=jax.ShapeDtypeStruct((2, rows, samples), jnp.float32),
        grid_spec=pltpu.PrefetchScalarGridSpec(
            num_scalar_prefetch=1,
            grid=(tiles, elems // tk),
            in_specs=[
                pl.BlockSpec((2, bt, tk), lambda i, k, h: (0, h[0] * tiles + i, k)),
                pl.BlockSpec((2, tk, samples), lambda i, k, h: (0, k, 0)),
            ],
            out_specs=pl.BlockSpec((2, bt, samples), lambda i, k, h: (0, i, 0)),
        ),
        compiler_params=pltpu.CompilerParams(
            dimension_semantics=("arbitrary", "arbitrary"), vmem_limit_bytes=48 * 1024 * 1024
        ),
        cost_estimate=pl.CostEstimate(
            flops=8 * rows * elems * samples,
            transcendentals=0,
            bytes_accessed=4 * rows * elems + 4 * elems * samples * tiles + 8 * rows * samples,
        ),
    )(half, w, x)


def block_kernel(index_ref, w_ref, x_ref, o_ref, acc_ref):
    bt = w_ref.shape[1]
    rows = w_ref[...].reshape(2 * bt, w_ref.shape[2])
    with_re = jnp.dot(rows, x_ref[0], preferred_element_type=jnp.float32)
    with_im = jnp.dot(rows, x_ref[1], preferred_element_type=jnp.float32)
    real = with_re[:bt] + with_im[bt:]
    imag = with_im[:bt] - with_re[bt:]
    step = pl.program_id(0)

    @pl.when(step == 0)
    def _():
        acc_ref[0] = real
        acc_ref[1] = imag

    @pl.when(step > 0)
    def _():
        acc_ref[0] += real
        acc_ref[1] += imag

    @pl.when(step == pl.num_programs(0) - 1)
    def _():
        o_ref[0] = acc_ref[0].T
        o_ref[1] = acc_ref[1].T


def block_partial(signal, weights, index, count):
    w = weights[:, 0]
    x = signal[:, 0]
    elems = w.shape[2]
    samples = x.shape[2]
    tk = min(ELEM_TILE, elems)
    return pl.pallas_call(
        block_kernel,
        out_shape=jax.ShapeDtypeStruct((2, samples, count), jnp.float32),
        grid_spec=pltpu.PrefetchScalarGridSpec(
            num_scalar_prefetch=1,
            grid=(elems // tk,),
            in_specs=[
                pl.BlockSpec((2, count, tk), lambda k, b: (0, b[0], k)),
                pl.BlockSpec((2, tk, samples), lambda k, b: (0, k, 0)),
            ],
            out_specs=pl.BlockSpec((2, samples, count), lambda k, b: (0, 0, 0)),
            scratch_shapes=[pltpu.VMEM((2, count, samples), jnp.float32)],
        ),
        compiler_params=pltpu.CompilerParams(
            dimension_semantics=("arbitrary",), vmem_limit_bytes=48 * 1024 * 1024
        ),
        cost_estimate=pl.CostEstimate(
            flops=8 * count * elems * samples,
            transcendentals=0,
            bytes_accessed=4 * count * elems + 4 * elems * samples + 8 * count * samples,
        ),
    )(index.reshape(1), w, x)


def send_plan(n_elem):
    plan = []
    serves = []
    for step in range(1, n_elem):
        right = {c: c + n_elem - step for c in range(step)}
        left = {c: c - n_elem + step for c in range(n_elem - step, n_elem)}
        if set(right) & set(left):
            plan += [right, left]
            serves += [(step, "right"), (step, "left")]
        else:
            plan.append({**right, **left})
            serves.append((step, "both"))
    own_call = {}
    for c in range(n_elem):
        free = [k for k, row in enumerate(plan) if c not in row]
        if free:
            plan[free[0]][c] = c
            own_call[c] = free[0]
        else:
            plan.append({c: c})
            serves.append((None, "own"))
            own_call[c] = len(plan) - 1
    table = [[row.get(c, c) for c in range(n_elem)] for row in plan]
    return table, serves, own_call


def line_scatter(signal, weights, n_elem):
    me = lax.axis_index("elem")
    local = weights.shape[2] // n_elem
    table, serves, own_call = send_plan(n_elem)
    made = []
    for row in table:
        index = jnp.asarray(row, jnp.int32)[me]
        made.append(jnp.swapaxes(block_partial(signal, weights, index, local), 1, 2))
    got_right = None
    got_left = None
    for step in range(1, n_elem):
        calls = {way: k for k, (s, way) in enumerate(serves) if s == step}
        to_right = made[calls.get("right", calls.get("both"))]
        to_left = made[calls.get("left", calls.get("both"))]
        if got_right is not None:
            to_right = to_right + got_right
            to_left = to_left + got_left
        got_right = lax.ppermute(to_right, "elem", [(c, c + 1) for c in range(step)])
        got_left = lax.ppermute(to_left, "elem", [(c, c - 1) for c in range(n_elem - step, n_elem)])
    own_at = jnp.asarray([own_call[c] for c in range(n_elem)], jnp.int32)[me]
    used = sorted(set(own_call.values()))
    own = made[used[0]]
    for k in used[1:]:
        own = jnp.where(own_at == k, made[k], own)
    return own + got_right + got_left


def on_device(signal, weights):
    n_elem = lax.axis_size("elem")
    samples = signal.shape[3]
    gates = samples // PULSES
    beams = weights.shape[2]
    if n_elem in (2, 4):
        summed = line_scatter(signal, weights, n_elem)
    else:
        part = partials(signal, weights)
        summed = lax.psum_scatter(part, "elem", scatter_dimension=1, tiled=True)
    stats = beam_stats(summed, gates)
    padded = with_halo(stats, "gate", 2)
    smoothed = (padded[..., :-2] + 2.0 * padded[..., 1:-1] + padded[..., 2:]) * 0.25
    power = smoothed[0]
    magnitude = jnp.sqrt(smoothed[1] * smoothed[1] + smoothed[2] * smoothed[2])
    floor_mag = jnp.maximum(magnitude, 0.25 * power)
    moments = jnp.stack(
        [
            10.0 * jnp.log10(power + 1e-06),
            smoothed[1] / floor_mag,
            smoothed[2] / floor_mag,
            jnp.log(power / floor_mag),
        ]
    )
    zdr = 10.0 * jnp.log10((smoothed[3] + 1e-06) / (smoothed[4] + 1e-06))
    corr = jnp.sqrt(smoothed[5] * smoothed[5] + smoothed[6] * smoothed[6]) / jnp.sqrt(
        smoothed[3] * smoothed[4]
    )
    pol_index = lax.axis_index("pol")
    polar = jnp.where(pol_index == 0, zdr, corr)
    return (moments[:, None], polar[None])


def solution(mesh):
    return jax.shard_map(
        on_device,
        mesh=mesh,
        in_specs=(P("arrays", "pol", "elem", "gate"), P("arrays", "pol", None, "elem")),
        out_specs=(
            P(None, ("arrays", "pol"), "elem", "gate"),
            P("pol", ("arrays", "elem"), "gate"),
        ),
        check_vma=False,
    )
```

```python
import jax
import jax.numpy as jnp
from jax import lax
from jax.experimental import pallas as pl
from jax.experimental.pallas import tpu as pltpu
from jax.sharding import PartitionSpec as P

PULSES = 64
BEAM_TILE = 512
ELEM_TILE = 1024


def swapped(value, axis, bit):
    mask = 2**bit
    pairs = [(source, source ^ mask) for source in range(lax.axis_size(axis))]
    return lax.ppermute(value, axis, pairs)


def with_halo(block, axis, dim):
    count = lax.axis_size(axis)
    first = lax.slice_in_dim(block, 0, 1, axis=dim)
    last = lax.slice_in_dim(block, block.shape[dim] - 1, None, axis=dim)
    index = lax.axis_index(axis)
    if count == 2:
        sent = jnp.where(index == 0, last, first)
        got = lax.ppermute(sent, axis, [(0, 1), (1, 0)])
        zero = jnp.zeros_like(got)
        low = jnp.where(index == 0, zero, got)
        high = jnp.where(index == 0, got, zero)
    else:
        forward = [(i, i + 1) for i in range(count - 1)]
        backward = [(target, source) for source, target in forward]
        low = lax.ppermute(last, axis, forward)
        high = lax.ppermute(first, axis, backward)
    return jnp.concatenate([low, block, high], axis=dim)


def lag_stats(real, imag):
    zero_lag = jnp.mean(real * real + imag * imag, axis=-1)
    lag_re = jnp.sum(real[..., :-1] * real[..., 1:] + imag[..., :-1] * imag[..., 1:], axis=-1) / (
        PULSES - 1
    )
    lag_im = jnp.sum(real[..., :-1] * imag[..., 1:] - imag[..., :-1] * real[..., 1:], axis=-1) / (
        PULSES - 1
    )
    return (zero_lag, lag_re, lag_im)


def pair_stats(first, second):
    power_h = jnp.mean(first[0] * first[0] + first[1] * first[1], axis=-1)
    power_v = jnp.mean(second[0] * second[0] + second[1] * second[1], axis=-1)
    cross_re = jnp.mean(first[0] * second[0] + first[1] * second[1], axis=-1)
    cross_im = jnp.mean(first[0] * second[1] - first[1] * second[0], axis=-1)
    return (power_h, power_v, cross_re, cross_im)


def beam_stats(summed, gates):
    count = summed.shape[1]
    real = summed[0].reshape(count, gates, PULSES)
    imag = summed[1].reshape(count, gates, PULSES)
    zero_lag, lag_re, lag_im = lag_stats(real, imag)
    series = jnp.stack([real, imag])
    pol_index = lax.axis_index("pol")
    other = swapped(series, "pol", 0)
    first = jnp.where(pol_index == 0, series, other)
    second = jnp.where(pol_index == 0, other, series)
    pair = jnp.stack(pair_stats(first, second))
    return jnp.concatenate([jnp.stack([zero_lag, lag_re, lag_im]), pair], axis=0)


def complex_kernel(half_ref, w_ref, x_ref, o_ref):
    bt = w_ref.shape[1]
    rows = w_ref[...].reshape(2 * bt, w_ref.shape[2])
    with_re = jnp.dot(rows, x_ref[0], preferred_element_type=jnp.float32)
    with_im = jnp.dot(rows, x_ref[1], preferred_element_type=jnp.float32)
    real = with_re[:bt] + with_im[bt:]
    imag = with_im[:bt] - with_re[bt:]

    @pl.when(pl.program_id(1) == 0)
    def _():
        o_ref[0] = real
        o_ref[1] = imag

    @pl.when(pl.program_id(1) > 0)
    def _():
        o_ref[0] += real
        o_ref[1] += imag


def partials(signal, weights, half=None):
    w = weights[:, 0]
    x = signal[:, 0]
    beams, elems = w.shape[1], w.shape[2]
    samples = x.shape[2]
    rows = beams if half is None else beams // 2
    bt = min(BEAM_TILE, rows)
    tk = min(ELEM_TILE, elems)
    tiles = rows // bt
    if half is None:
        half = jnp.zeros((1,), jnp.int32)
    return pl.pallas_call(
        complex_kernel,
        out_shape=jax.ShapeDtypeStruct((2, rows, samples), jnp.float32),
        grid_spec=pltpu.PrefetchScalarGridSpec(
            num_scalar_prefetch=1,
            grid=(tiles, elems // tk),
            in_specs=[
                pl.BlockSpec((2, bt, tk), lambda i, k, h: (0, h[0] * tiles + i, k)),
                pl.BlockSpec((2, tk, samples), lambda i, k, h: (0, k, 0)),
            ],
            out_specs=pl.BlockSpec((2, bt, samples), lambda i, k, h: (0, i, 0)),
        ),
        compiler_params=pltpu.CompilerParams(
            dimension_semantics=("arbitrary", "arbitrary"), vmem_limit_bytes=48 * 1024 * 1024
        ),
        cost_estimate=pl.CostEstimate(
            flops=8 * rows * elems * samples,
            transcendentals=0,
            bytes_accessed=4 * rows * elems + 4 * elems * samples * tiles + 8 * rows * samples,
        ),
    )(half, w, x)


def block_kernel(index_ref, w_ref, x_ref, o_ref, acc_ref):
    bt = w_ref.shape[1]
    rows = w_ref[...].reshape(2 * bt, w_ref.shape[2])
    with_re = jnp.dot(rows, x_ref[0], preferred_element_type=jnp.float32)
    with_im = jnp.dot(rows, x_ref[1], preferred_element_type=jnp.float32)
    real = with_re[:bt] + with_im[bt:]
    imag = with_im[:bt] - with_re[bt:]
    step = pl.program_id(0)

    @pl.when(step == 0)
    def _():
        acc_ref[0] = real
        acc_ref[1] = imag

    @pl.when(step > 0)
    def _():
        acc_ref[0] += real
        acc_ref[1] += imag

    @pl.when(step == pl.num_programs(0) - 1)
    def _():
        o_ref[0] = acc_ref[0].T
        o_ref[1] = acc_ref[1].T


def block_partial(signal, weights, index, count):
    w = weights[:, 0]
    x = signal[:, 0]
    elems = w.shape[2]
    samples = x.shape[2]
    tk = min(ELEM_TILE, elems)
    return pl.pallas_call(
        block_kernel,
        out_shape=jax.ShapeDtypeStruct((2, samples, count), jnp.float32),
        grid_spec=pltpu.PrefetchScalarGridSpec(
            num_scalar_prefetch=1,
            grid=(elems // tk,),
            in_specs=[
                pl.BlockSpec((2, count, tk), lambda k, b: (0, b[0], k)),
                pl.BlockSpec((2, tk, samples), lambda k, b: (0, k, 0)),
            ],
            out_specs=pl.BlockSpec((2, samples, count), lambda k, b: (0, 0, 0)),
            scratch_shapes=[pltpu.VMEM((2, count, samples), jnp.float32)],
        ),
        compiler_params=pltpu.CompilerParams(
            dimension_semantics=("arbitrary",), vmem_limit_bytes=48 * 1024 * 1024
        ),
        cost_estimate=pl.CostEstimate(
            flops=8 * count * elems * samples,
            transcendentals=0,
            bytes_accessed=4 * count * elems + 4 * elems * samples + 8 * count * samples,
        ),
    )(index.reshape(1), w, x)


def send_plan(n_elem):
    plan = []
    serves = []
    for step in range(1, n_elem):
        right = {c: c + n_elem - step for c in range(step)}
        left = {c: c - n_elem + step for c in range(n_elem - step, n_elem)}
        if set(right) & set(left):
            plan += [right, left]
            serves += [(step, "right"), (step, "left")]
        else:
            plan.append({**right, **left})
            serves.append((step, "both"))
    own_call = {}
    for c in range(n_elem):
        free = [k for k, row in enumerate(plan) if c not in row]
        if free:
            plan[free[0]][c] = c
            own_call[c] = free[0]
        else:
            plan.append({c: c})
            serves.append((None, "own"))
            own_call[c] = len(plan) - 1
    table = [[row.get(c, c) for c in range(n_elem)] for row in plan]
    return table, serves, own_call


def line_scatter(signal, weights, n_elem):
    me = lax.axis_index("elem")
    local = weights.shape[2] // n_elem
    table, serves, own_call = send_plan(n_elem)
    made = []
    def lookup(row):
        value = jnp.int32(row[0])
        for c in range(1, n_elem):
            value = jnp.where(me == c, jnp.int32(row[c]), value)
        return value

    for row in table:
        index = lookup(row)
        made.append(jnp.swapaxes(block_partial(signal, weights, index, local), 1, 2))
    got_right = None
    got_left = None
    for step in range(1, n_elem):
        calls = {way: k for k, (s, way) in enumerate(serves) if s == step}
        to_right = made[calls.get("right", calls.get("both"))]
        to_left = made[calls.get("left", calls.get("both"))]
        if got_right is not None:
            to_right = to_right + got_right
            to_left = to_left + got_left
        got_right = lax.ppermute(to_right, "elem", [(c, c + 1) for c in range(step)])
        got_left = lax.ppermute(to_left, "elem", [(c, c - 1) for c in range(n_elem - step, n_elem)])
    own_at = lookup([own_call[c] for c in range(n_elem)])
    used = sorted(set(own_call.values()))
    own = made[used[0]]
    for k in used[1:]:
        own = jnp.where(own_at == k, made[k], own)
    return own + got_right + got_left


def on_device(signal, weights):
    n_elem = lax.axis_size("elem")
    samples = signal.shape[3]
    gates = samples // PULSES
    beams = weights.shape[2]
    if n_elem in (2, 4):
        summed = line_scatter(signal, weights, n_elem)
    else:
        part = partials(signal, weights)
        summed = lax.psum_scatter(part, "elem", scatter_dimension=1, tiled=True)
    stats = beam_stats(summed, gates)
    padded = with_halo(stats, "gate", 2)
    smoothed = (padded[..., :-2] + 2.0 * padded[..., 1:-1] + padded[..., 2:]) * 0.25
    power = smoothed[0]
    magnitude = jnp.sqrt(smoothed[1] * smoothed[1] + smoothed[2] * smoothed[2])
    floor_mag = jnp.maximum(magnitude, 0.25 * power)
    moments = jnp.stack(
        [
            10.0 * jnp.log10(power + 1e-06),
            smoothed[1] / floor_mag,
            smoothed[2] / floor_mag,
            jnp.log(power / floor_mag),
        ]
    )
    zdr = 10.0 * jnp.log10((smoothed[3] + 1e-06) / (smoothed[4] + 1e-06))
    corr = jnp.sqrt(smoothed[5] * smoothed[5] + smoothed[6] * smoothed[6]) / jnp.sqrt(
        smoothed[3] * smoothed[4]
    )
    pol_index = lax.axis_index("pol")
    polar = jnp.where(pol_index == 0, zdr, corr)
    return (moments[:, None], polar[None])


def solution(mesh):
    return jax.shard_map(
        on_device,
        mesh=mesh,
        in_specs=(P("arrays", "pol", "elem", "gate"), P("arrays", "pol", None, "elem")),
        out_specs=(
            P(None, ("arrays", "pol"), "elem", "gate"),
            P("pol", ("arrays", "elem"), "gate"),
        ),
        check_vma=False,
    )
```

```python
import jax
import jax.numpy as jnp
from jax import lax
from jax.experimental import pallas as pl
from jax.experimental.pallas import tpu as pltpu
from jax.sharding import PartitionSpec as P

PULSES = 64
BEAM_TILE = 512
ELEM_TILE = 1024


def swapped(value, axis, bit):
    mask = 2**bit
    pairs = [(source, source ^ mask) for source in range(lax.axis_size(axis))]
    return lax.ppermute(value, axis, pairs)


def with_halo(block, axis, dim):
    count = lax.axis_size(axis)
    first = lax.slice_in_dim(block, 0, 1, axis=dim)
    last = lax.slice_in_dim(block, block.shape[dim] - 1, None, axis=dim)
    index = lax.axis_index(axis)
    if count == 2:
        sent = jnp.where(index == 0, last, first)
        got = lax.ppermute(sent, axis, [(0, 1), (1, 0)])
        zero = jnp.zeros_like(got)
        low = jnp.where(index == 0, zero, got)
        high = jnp.where(index == 0, got, zero)
    else:
        forward = [(i, i + 1) for i in range(count - 1)]
        backward = [(target, source) for source, target in forward]
        low = lax.ppermute(last, axis, forward)
        high = lax.ppermute(first, axis, backward)
    return jnp.concatenate([low, block, high], axis=dim)


def lag_stats(real, imag):
    zero_lag = jnp.mean(real * real + imag * imag, axis=-1)
    lag_re = jnp.sum(real[..., :-1] * real[..., 1:] + imag[..., :-1] * imag[..., 1:], axis=-1) / (
        PULSES - 1
    )
    lag_im = jnp.sum(real[..., :-1] * imag[..., 1:] - imag[..., :-1] * real[..., 1:], axis=-1) / (
        PULSES - 1
    )
    return (zero_lag, lag_re, lag_im)


def pair_stats(first, second):
    power_h = jnp.mean(first[0] * first[0] + first[1] * first[1], axis=-1)
    power_v = jnp.mean(second[0] * second[0] + second[1] * second[1], axis=-1)
    cross_re = jnp.mean(first[0] * second[0] + first[1] * second[1], axis=-1)
    cross_im = jnp.mean(first[0] * second[1] - first[1] * second[0], axis=-1)
    return (power_h, power_v, cross_re, cross_im)


def beam_stats(summed, gates):
    count = summed.shape[1]
    real = summed[0].reshape(count, gates, PULSES)
    imag = summed[1].reshape(count, gates, PULSES)
    zero_lag, lag_re, lag_im = lag_stats(real, imag)
    series = jnp.stack([real, imag])
    pol_index = lax.axis_index("pol")
    other = swapped(series, "pol", 0)
    first = jnp.where(pol_index == 0, series, other)
    second = jnp.where(pol_index == 0, other, series)
    pair = jnp.stack(pair_stats(first, second))
    return jnp.concatenate([jnp.stack([zero_lag, lag_re, lag_im]), pair], axis=0)


def complex_kernel(half_ref, w_ref, x_ref, o_ref):
    bt = w_ref.shape[1]
    rows = w_ref[...].reshape(2 * bt, w_ref.shape[2])
    with_re = jnp.dot(rows, x_ref[0], preferred_element_type=jnp.float32)
    with_im = jnp.dot(rows, x_ref[1], preferred_element_type=jnp.float32)
    real = with_re[:bt] + with_im[bt:]
    imag = with_im[:bt] - with_re[bt:]

    @pl.when(pl.program_id(1) == 0)
    def _():
        o_ref[0] = real
        o_ref[1] = imag

    @pl.when(pl.program_id(1) > 0)
    def _():
        o_ref[0] += real
        o_ref[1] += imag


def partials(signal, weights, half=None):
    w = weights[:, 0]
    x = signal[:, 0]
    beams, elems = w.shape[1], w.shape[2]
    samples = x.shape[2]
    rows = beams if half is None else beams // 2
    bt = min(BEAM_TILE, rows)
    tk = min(ELEM_TILE, elems)
    tiles = rows // bt
    if half is None:
        half = jnp.zeros((1,), jnp.int32)
    return pl.pallas_call(
        complex_kernel,
        out_shape=jax.ShapeDtypeStruct((2, rows, samples), jnp.float32),
        grid_spec=pltpu.PrefetchScalarGridSpec(
            num_scalar_prefetch=1,
            grid=(tiles, elems // tk),
            in_specs=[
                pl.BlockSpec((2, bt, tk), lambda i, k, h: (0, h[0] * tiles + i, k)),
                pl.BlockSpec((2, tk, samples), lambda i, k, h: (0, k, 0)),
            ],
            out_specs=pl.BlockSpec((2, bt, samples), lambda i, k, h: (0, i, 0)),
        ),
        compiler_params=pltpu.CompilerParams(
            dimension_semantics=("arbitrary", "arbitrary"), vmem_limit_bytes=48 * 1024 * 1024
        ),
        cost_estimate=pl.CostEstimate(
            flops=8 * rows * elems * samples,
            transcendentals=0,
            bytes_accessed=4 * rows * elems + 4 * elems * samples * tiles + 8 * rows * samples,
        ),
    )(half, w, x)


def block_kernel(index_ref, w_ref, x_ref, o_ref, acc_ref):
    bt = w_ref.shape[1]
    rows = w_ref[...].reshape(2 * bt, w_ref.shape[2])
    with_re = jnp.dot(rows, x_ref[0], preferred_element_type=jnp.float32)
    with_im = jnp.dot(rows, x_ref[1], preferred_element_type=jnp.float32)
    real = with_re[:bt] + with_im[bt:]
    imag = with_im[:bt] - with_re[bt:]
    step = pl.program_id(0)

    @pl.when(step == 0)
    def _():
        acc_ref[0] = real
        acc_ref[1] = imag

    @pl.when(step > 0)
    def _():
        acc_ref[0] += real
        acc_ref[1] += imag

    @pl.when(step == pl.num_programs(0) - 1)
    def _():
        o_ref[0] = acc_ref[0].T
        o_ref[1] = acc_ref[1].T


def block_partial(signal, weights, index, count):
    w = weights[:, 0]
    x = signal[:, 0]
    elems = w.shape[2]
    samples = x.shape[2]
    tk = min(ELEM_TILE, elems)
    return pl.pallas_call(
        block_kernel,
        out_shape=jax.ShapeDtypeStruct((2, samples, count), jnp.float32),
        grid_spec=pltpu.PrefetchScalarGridSpec(
            num_scalar_prefetch=1,
            grid=(elems // tk,),
            in_specs=[
                pl.BlockSpec((2, count, tk), lambda k, b: (0, b[0], k)),
                pl.BlockSpec((2, tk, samples), lambda k, b: (0, k, 0)),
            ],
            out_specs=pl.BlockSpec((2, samples, count), lambda k, b: (0, 0, 0)),
            scratch_shapes=[pltpu.VMEM((2, count, samples), jnp.float32)],
        ),
        compiler_params=pltpu.CompilerParams(
            dimension_semantics=("arbitrary",), vmem_limit_bytes=48 * 1024 * 1024
        ),
        cost_estimate=pl.CostEstimate(
            flops=8 * count * elems * samples,
            transcendentals=0,
            bytes_accessed=4 * count * elems + 4 * elems * samples + 8 * count * samples,
        ),
    )(index.reshape(1), w, x)


def send_plan(n_elem):
    plan = []
    serves = []
    for step in range(1, n_elem):
        right = {c: c + n_elem - step for c in range(step)}
        left = {c: c - n_elem + step for c in range(n_elem - step, n_elem)}
        if set(right) & set(left):
            plan += [right, left]
            serves += [(step, "right"), (step, "left")]
        else:
            plan.append({**right, **left})
            serves.append((step, "both"))
    own_call = {}
    for c in range(n_elem):
        free = [k for k, row in enumerate(plan) if c not in row]
        if free:
            plan[free[0]][c] = c
            own_call[c] = free[0]
        else:
            plan.append({c: c})
            serves.append((None, "own"))
            own_call[c] = len(plan) - 1
    table = [[row.get(c, c) for c in range(n_elem)] for row in plan]
    return table, serves, own_call


def line_scatter(signal, weights, n_elem):
    me = lax.axis_index("elem")
    local = weights.shape[2] // n_elem
    table, serves, own_call = send_plan(n_elem)
    made = []
    for k, row in enumerate(table):
        if k == 0 and row == [n_elem - 1] + list(range(1, n_elem - 1)) + [0]:
            index = jnp.where(me == 0, n_elem - 1, jnp.where(me == n_elem - 1, 0, me)).astype(jnp.int32)
        else:
            index = jnp.asarray(row, jnp.int32)[me]
        made.append(jnp.swapaxes(block_partial(signal, weights, index, local), 1, 2))
    got_right = None
    got_left = None
    for step in range(1, n_elem):
        calls = {way: k for k, (s, way) in enumerate(serves) if s == step}
        to_right = made[calls.get("right", calls.get("both"))]
        to_left = made[calls.get("left", calls.get("both"))]
        if got_right is not None:
            to_right = to_right + got_right
            to_left = to_left + got_left
        got_right = lax.ppermute(to_right, "elem", [(c, c + 1) for c in range(step)])
        got_left = lax.ppermute(to_left, "elem", [(c, c - 1) for c in range(n_elem - step, n_elem)])
    own_at = jnp.asarray([own_call[c] for c in range(n_elem)], jnp.int32)[me]
    used = sorted(set(own_call.values()))
    own = made[used[0]]
    for k in used[1:]:
        own = jnp.where(own_at == k, made[k], own)
    return own + got_right + got_left


def on_device(signal, weights):
    n_elem = lax.axis_size("elem")
    samples = signal.shape[3]
    gates = samples // PULSES
    beams = weights.shape[2]
    if n_elem in (2, 4):
        summed = line_scatter(signal, weights, n_elem)
    else:
        part = partials(signal, weights)
        summed = lax.psum_scatter(part, "elem", scatter_dimension=1, tiled=True)
    stats = beam_stats(summed, gates)
    padded = with_halo(stats, "gate", 2)
    smoothed = (padded[..., :-2] + 2.0 * padded[..., 1:-1] + padded[..., 2:]) * 0.25
    power = smoothed[0]
    magnitude = jnp.sqrt(smoothed[1] * smoothed[1] + smoothed[2] * smoothed[2])
    floor_mag = jnp.maximum(magnitude, 0.25 * power)
    moments = jnp.stack(
        [
            10.0 * jnp.log10(power + 1e-06),
            smoothed[1] / floor_mag,
            smoothed[2] / floor_mag,
            jnp.log(power / floor_mag),
        ]
    )
    zdr = 10.0 * jnp.log10((smoothed[3] + 1e-06) / (smoothed[4] + 1e-06))
    corr = jnp.sqrt(smoothed[5] * smoothed[5] + smoothed[6] * smoothed[6]) / jnp.sqrt(
        smoothed[3] * smoothed[4]
    )
    pol_index = lax.axis_index("pol")
    polar = jnp.where(pol_index == 0, zdr, corr)
    return (moments[:, None], polar[None])


def solution(mesh):
    return jax.shard_map(
        on_device,
        mesh=mesh,
        in_specs=(P("arrays", "pol", "elem", "gate"), P("arrays", "pol", None, "elem")),
        out_specs=(
            P(None, ("arrays", "pol"), "elem", "gate"),
            P("pol", ("arrays", "elem"), "gate"),
        ),
        check_vma=False,
    )
```

```python
import jax
import jax.numpy as jnp
from jax import lax
from jax.experimental import pallas as pl
from jax.experimental.pallas import tpu as pltpu
from jax.sharding import PartitionSpec as P

PULSES = 64
BEAM_TILE = 512
ELEM_TILE = 1024


def swapped(value, axis, bit):
    mask = 2**bit
    pairs = [(source, source ^ mask) for source in range(lax.axis_size(axis))]
    return lax.ppermute(value, axis, pairs)


def with_halo(block, axis, dim):
    count = lax.axis_size(axis)
    first = lax.slice_in_dim(block, 0, 1, axis=dim)
    last = lax.slice_in_dim(block, block.shape[dim] - 1, None, axis=dim)
    index = lax.axis_index(axis)
    if count == 2:
        sent = jnp.where(index == 0, last, first)
        got = lax.ppermute(sent, axis, [(0, 1), (1, 0)])
        zero = jnp.zeros_like(got)
        low = jnp.where(index == 0, zero, got)
        high = jnp.where(index == 0, got, zero)
    else:
        forward = [(i, i + 1) for i in range(count - 1)]
        backward = [(target, source) for source, target in forward]
        low = lax.ppermute(last, axis, forward)
        high = lax.ppermute(first, axis, backward)
    return jnp.concatenate([low, block, high], axis=dim)


def lag_stats(real, imag):
    zero_lag = jnp.mean(real * real + imag * imag, axis=-1)
    lag_re = jnp.sum(real[..., :-1] * real[..., 1:] + imag[..., :-1] * imag[..., 1:], axis=-1) / (
        PULSES - 1
    )
    lag_im = jnp.sum(real[..., :-1] * imag[..., 1:] - imag[..., :-1] * real[..., 1:], axis=-1) / (
        PULSES - 1
    )
    return (zero_lag, lag_re, lag_im)


def pair_stats(first, second):
    power_h = jnp.mean(first[0] * first[0] + first[1] * first[1], axis=-1)
    power_v = jnp.mean(second[0] * second[0] + second[1] * second[1], axis=-1)
    cross_re = jnp.mean(first[0] * second[0] + first[1] * second[1], axis=-1)
    cross_im = jnp.mean(first[0] * second[1] - first[1] * second[0], axis=-1)
    return (power_h, power_v, cross_re, cross_im)


def beam_stats(summed, gates):
    count = summed.shape[1]
    real = summed[0].reshape(count, gates, PULSES)
    imag = summed[1].reshape(count, gates, PULSES)
    zero_lag, lag_re, lag_im = lag_stats(real, imag)
    series = jnp.stack([real, imag])
    pol_index = lax.axis_index("pol")
    other = swapped(series, "pol", 0)
    first = jnp.where(pol_index == 0, series, other)
    second = jnp.where(pol_index == 0, other, series)
    pair = jnp.stack(pair_stats(first, second))
    return jnp.concatenate([jnp.stack([zero_lag, lag_re, lag_im]), pair], axis=0)


def complex_kernel(half_ref, w_ref, x_ref, o_ref):
    bt = w_ref.shape[1]
    rows = w_ref[...].reshape(2 * bt, w_ref.shape[2])
    with_re = jnp.dot(rows, x_ref[0], preferred_element_type=jnp.float32)
    with_im = jnp.dot(rows, x_ref[1], preferred_element_type=jnp.float32)
    real = with_re[:bt] + with_im[bt:]
    imag = with_im[:bt] - with_re[bt:]

    @pl.when(pl.program_id(1) == 0)
    def _():
        o_ref[0] = real
        o_ref[1] = imag

    @pl.when(pl.program_id(1) > 0)
    def _():
        o_ref[0] += real
        o_ref[1] += imag


def partials(signal, weights, half=None):
    w = weights[:, 0]
    x = signal[:, 0]
    beams, elems = w.shape[1], w.shape[2]
    samples = x.shape[2]
    rows = beams if half is None else beams // 2
    bt = min(BEAM_TILE, rows)
    tk = min(ELEM_TILE, elems)
    tiles = rows // bt
    if half is None:
        half = jnp.zeros((1,), jnp.int32)
    return pl.pallas_call(
        complex_kernel,
        out_shape=jax.ShapeDtypeStruct((2, rows, samples), jnp.float32),
        grid_spec=pltpu.PrefetchScalarGridSpec(
            num_scalar_prefetch=1,
            grid=(tiles, elems // tk),
            in_specs=[
                pl.BlockSpec((2, bt, tk), lambda i, k, h: (0, h[0] * tiles + i, k)),
                pl.BlockSpec((2, tk, samples), lambda i, k, h: (0, k, 0)),
            ],
            out_specs=pl.BlockSpec((2, bt, samples), lambda i, k, h: (0, i, 0)),
        ),
        compiler_params=pltpu.CompilerParams(
            dimension_semantics=("arbitrary", "arbitrary"), vmem_limit_bytes=48 * 1024 * 1024
        ),
        cost_estimate=pl.CostEstimate(
            flops=8 * rows * elems * samples,
            transcendentals=0,
            bytes_accessed=4 * rows * elems + 4 * elems * samples * tiles + 8 * rows * samples,
        ),
    )(half, w, x)


def block_kernel(index_ref, w_ref, x_ref, o_ref, acc_ref):
    bt = w_ref.shape[1]
    rows = w_ref[...].reshape(2 * bt, w_ref.shape[2])
    with_re = jnp.dot(rows, x_ref[0], preferred_element_type=jnp.float32)
    with_im = jnp.dot(rows, x_ref[1], preferred_element_type=jnp.float32)
    real = with_re[:bt] + with_im[bt:]
    imag = with_im[:bt] - with_re[bt:]
    step = pl.program_id(0)

    @pl.when(step == 0)
    def _():
        acc_ref[0] = real
        acc_ref[1] = imag

    @pl.when(step > 0)
    def _():
        acc_ref[0] += real
        acc_ref[1] += imag

    @pl.when(step == pl.num_programs(0) - 1)
    def _():
        o_ref[0] = acc_ref[0].T
        o_ref[1] = acc_ref[1].T


def block_partial(signal, weights, index, count):
    w = weights[:, 0]
    x = signal[:, 0]
    elems = w.shape[2]
    samples = x.shape[2]
    tk = min(ELEM_TILE, elems)
    return pl.pallas_call(
        block_kernel,
        out_shape=jax.ShapeDtypeStruct((2, samples, count), jnp.float32),
        grid_spec=pltpu.PrefetchScalarGridSpec(
            num_scalar_prefetch=1,
            grid=(elems // tk,),
            in_specs=[
                pl.BlockSpec((2, count, tk), lambda k, b: (0, b[0], k)),
                pl.BlockSpec((2, tk, samples), lambda k, b: (0, k, 0)),
            ],
            out_specs=pl.BlockSpec((2, samples, count), lambda k, b: (0, 0, 0)),
            scratch_shapes=[pltpu.VMEM((2, count, samples), jnp.float32)],
        ),
        compiler_params=pltpu.CompilerParams(
            dimension_semantics=("arbitrary",), vmem_limit_bytes=48 * 1024 * 1024
        ),
        cost_estimate=pl.CostEstimate(
            flops=8 * count * elems * samples,
            transcendentals=0,
            bytes_accessed=4 * count * elems + 4 * elems * samples + 8 * count * samples,
        ),
    )(index.reshape(1), w, x)


def send_plan(n_elem):
    plan = []
    serves = []
    for step in range(1, n_elem):
        right = {c: c + n_elem - step for c in range(step)}
        left = {c: c - n_elem + step for c in range(n_elem - step, n_elem)}
        if set(right) & set(left):
            plan += [right, left]
            serves += [(step, "right"), (step, "left")]
        else:
            plan.append({**right, **left})
            serves.append((step, "both"))
    own_call = {}
    for c in range(n_elem):
        free = [k for k, row in enumerate(plan) if c not in row]
        if free:
            plan[free[0]][c] = c
            own_call[c] = free[0]
        else:
            plan.append({c: c})
            serves.append((None, "own"))
            own_call[c] = len(plan) - 1
    table = [[row.get(c, c) for c in range(n_elem)] for row in plan]
    return table, serves, own_call


def line_scatter(signal, weights, n_elem):
    me = lax.axis_index("elem")
    local = weights.shape[2] // n_elem
    table, serves, own_call = send_plan(n_elem)
    made = []
    later = jnp.asarray(table, jnp.int32)[:, me]
    for k, row in enumerate(table):
        if k == 0 and row == [n_elem - 1] + list(range(1, n_elem - 1)) + [0]:
            index = jnp.where(me == 0, n_elem - 1, jnp.where(me == n_elem - 1, 0, me)).astype(jnp.int32)
        else:
            index = later[k]
        made.append(jnp.swapaxes(block_partial(signal, weights, index, local), 1, 2))
    got_right = None
    got_left = None
    for step in range(1, n_elem):
        calls = {way: k for k, (s, way) in enumerate(serves) if s == step}
        to_right = made[calls.get("right", calls.get("both"))]
        to_left = made[calls.get("left", calls.get("both"))]
        if got_right is not None:
            to_right = to_right + got_right
            to_left = to_left + got_left
        pairs_right = [(c, c + 1) for c in range(step)]
        pairs_left = [(c, c - 1) for c in range(n_elem - step, n_elem)]
        merged = pairs_right + pairs_left
        if "both" in calls and got_right is None and len({t for _, t in merged}) == len(merged):
            got_right = got_left = lax.ppermute(to_right, "elem", merged)
        else:
            got_right = lax.ppermute(to_right, "elem", pairs_right)
            got_left = lax.ppermute(to_left, "elem", pairs_left)
    own_at = jnp.asarray([own_call[c] for c in range(n_elem)], jnp.int32)[me]
    used = sorted(set(own_call.values()))
    own = made[used[0]]
    for k in used[1:]:
        own = jnp.where(own_at == k, made[k], own)
    return own + got_right + got_left


def on_device(signal, weights):
    n_elem = lax.axis_size("elem")
    samples = signal.shape[3]
    gates = samples // PULSES
    beams = weights.shape[2]
    if n_elem in (2, 4):
        summed = line_scatter(signal, weights, n_elem)
    else:
        part = partials(signal, weights)
        summed = lax.psum_scatter(part, "elem", scatter_dimension=1, tiled=True)
    stats = beam_stats(summed, gates)
    padded = with_halo(stats, "gate", 2)
    smoothed = (padded[..., :-2] + 2.0 * padded[..., 1:-1] + padded[..., 2:]) * 0.25
    power = smoothed[0]
    magnitude = jnp.sqrt(smoothed[1] * smoothed[1] + smoothed[2] * smoothed[2])
    floor_mag = jnp.maximum(magnitude, 0.25 * power)
    moments = jnp.stack(
        [
            10.0 * jnp.log10(power + 1e-06),
            smoothed[1] / floor_mag,
            smoothed[2] / floor_mag,
            jnp.log(power / floor_mag),
        ]
    )
    zdr = 10.0 * jnp.log10((smoothed[3] + 1e-06) / (smoothed[4] + 1e-06))
    corr = jnp.sqrt(smoothed[5] * smoothed[5] + smoothed[6] * smoothed[6]) / jnp.sqrt(
        smoothed[3] * smoothed[4]
    )
    pol_index = lax.axis_index("pol")
    polar = jnp.where(pol_index == 0, zdr, corr)
    return (moments[:, None], polar[None])


def solution(mesh):
    return jax.shard_map(
        on_device,
        mesh=mesh,
        in_specs=(P("arrays", "pol", "elem", "gate"), P("arrays", "pol", None, "elem")),
        out_specs=(
            P(None, ("arrays", "pol"), "elem", "gate"),
            P("pol", ("arrays", "elem"), "gate"),
        ),
        check_vma=False,
    )
```

```python
import jax
import jax.numpy as jnp
from jax import lax
from jax.experimental import pallas as pl
from jax.experimental.pallas import tpu as pltpu
from jax.sharding import PartitionSpec as P

PULSES = 64
BEAM_TILE = 512
ELEM_TILE = 1024


def swapped(value, axis, bit):
    mask = 2**bit
    pairs = [(source, source ^ mask) for source in range(lax.axis_size(axis))]
    return lax.ppermute(value, axis, pairs)


def with_halo(block, axis, dim):
    count = lax.axis_size(axis)
    first = lax.slice_in_dim(block, 0, 1, axis=dim)
    last = lax.slice_in_dim(block, block.shape[dim] - 1, None, axis=dim)
    index = lax.axis_index(axis)
    if count == 2:
        sent = jnp.where(index == 0, last, first)
        got = lax.ppermute(sent, axis, [(0, 1), (1, 0)])
        zero = jnp.zeros_like(got)
        low = jnp.where(index == 0, zero, got)
        high = jnp.where(index == 0, got, zero)
    else:
        forward = [(i, i + 1) for i in range(count - 1)]
        backward = [(target, source) for source, target in forward]
        low = lax.ppermute(last, axis, forward)
        high = lax.ppermute(first, axis, backward)
    return jnp.concatenate([low, block, high], axis=dim)


def lag_stats(real, imag):
    zero_lag = jnp.mean(real * real + imag * imag, axis=-1)
    lag_re = jnp.sum(real[..., :-1] * real[..., 1:] + imag[..., :-1] * imag[..., 1:], axis=-1) / (
        PULSES - 1
    )
    lag_im = jnp.sum(real[..., :-1] * imag[..., 1:] - imag[..., :-1] * real[..., 1:], axis=-1) / (
        PULSES - 1
    )
    return (zero_lag, lag_re, lag_im)


def pair_stats(first, second):
    power_h = jnp.mean(first[0] * first[0] + first[1] * first[1], axis=-1)
    power_v = jnp.mean(second[0] * second[0] + second[1] * second[1], axis=-1)
    cross_re = jnp.mean(first[0] * second[0] + first[1] * second[1], axis=-1)
    cross_im = jnp.mean(first[0] * second[1] - first[1] * second[0], axis=-1)
    return (power_h, power_v, cross_re, cross_im)


def beam_stats(summed, gates):
    count = summed.shape[1]
    real = summed[0].reshape(count, gates, PULSES)
    imag = summed[1].reshape(count, gates, PULSES)
    zero_lag, lag_re, lag_im = lag_stats(real, imag)
    series = jnp.stack([real, imag])
    pol_index = lax.axis_index("pol")
    other = swapped(series, "pol", 0)
    first = jnp.where(pol_index == 0, series, other)
    second = jnp.where(pol_index == 0, other, series)
    pair = jnp.stack(pair_stats(first, second))
    return jnp.concatenate([jnp.stack([zero_lag, lag_re, lag_im]), pair], axis=0)


def complex_kernel(half_ref, w_ref, x_ref, o_ref):
    bt = w_ref.shape[1]
    rows = w_ref[...].reshape(2 * bt, w_ref.shape[2])
    with_re = jnp.dot(rows, x_ref[0], preferred_element_type=jnp.float32)
    with_im = jnp.dot(rows, x_ref[1], preferred_element_type=jnp.float32)
    real = with_re[:bt] + with_im[bt:]
    imag = with_im[:bt] - with_re[bt:]

    @pl.when(pl.program_id(1) == 0)
    def _():
        o_ref[0] = real
        o_ref[1] = imag

    @pl.when(pl.program_id(1) > 0)
    def _():
        o_ref[0] += real
        o_ref[1] += imag


def partials(signal, weights, half=None):
    w = weights[:, 0]
    x = signal[:, 0]
    beams, elems = w.shape[1], w.shape[2]
    samples = x.shape[2]
    rows = beams if half is None else beams // 2
    bt = min(BEAM_TILE, rows)
    tk = min(ELEM_TILE, elems)
    tiles = rows // bt
    if half is None:
        half = jnp.zeros((1,), jnp.int32)
    return pl.pallas_call(
        complex_kernel,
        out_shape=jax.ShapeDtypeStruct((2, rows, samples), jnp.float32),
        grid_spec=pltpu.PrefetchScalarGridSpec(
            num_scalar_prefetch=1,
            grid=(tiles, elems // tk),
            in_specs=[
                pl.BlockSpec((2, bt, tk), lambda i, k, h: (0, h[0] * tiles + i, k)),
                pl.BlockSpec((2, tk, samples), lambda i, k, h: (0, k, 0)),
            ],
            out_specs=pl.BlockSpec((2, bt, samples), lambda i, k, h: (0, i, 0)),
        ),
        compiler_params=pltpu.CompilerParams(
            dimension_semantics=("arbitrary", "arbitrary"), vmem_limit_bytes=48 * 1024 * 1024
        ),
        cost_estimate=pl.CostEstimate(
            flops=8 * rows * elems * samples,
            transcendentals=0,
            bytes_accessed=4 * rows * elems + 4 * elems * samples * tiles + 8 * rows * samples,
        ),
    )(half, w, x)


def block_kernel(index_ref, w_ref, x_ref, o_ref, acc_ref):
    bt = w_ref.shape[1]
    rows = w_ref[...].reshape(2 * bt, w_ref.shape[2])
    with_re = jnp.dot(rows, x_ref[0], preferred_element_type=jnp.float32)
    with_im = jnp.dot(rows, x_ref[1], preferred_element_type=jnp.float32)
    real = with_re[:bt] + with_im[bt:]
    imag = with_im[:bt] - with_re[bt:]
    step = pl.program_id(0)

    @pl.when(step == 0)
    def _():
        acc_ref[0] = real
        acc_ref[1] = imag

    @pl.when(step > 0)
    def _():
        acc_ref[0] += real
        acc_ref[1] += imag

    @pl.when(step == pl.num_programs(0) - 1)
    def _():
        o_ref[0] = acc_ref[0].T
        o_ref[1] = acc_ref[1].T


def block_partial(signal, weights, index, count):
    w = weights[:, 0]
    x = signal[:, 0]
    elems = w.shape[2]
    samples = x.shape[2]
    tk = min(ELEM_TILE, elems)
    return pl.pallas_call(
        block_kernel,
        out_shape=jax.ShapeDtypeStruct((2, samples, count), jnp.float32),
        grid_spec=pltpu.PrefetchScalarGridSpec(
            num_scalar_prefetch=1,
            grid=(elems // tk,),
            in_specs=[
                pl.BlockSpec((2, count, tk), lambda k, b: (0, b[0], k)),
                pl.BlockSpec((2, tk, samples), lambda k, b: (0, k, 0)),
            ],
            out_specs=pl.BlockSpec((2, samples, count), lambda k, b: (0, 0, 0)),
            scratch_shapes=[pltpu.VMEM((2, count, samples), jnp.float32)],
        ),
        compiler_params=pltpu.CompilerParams(
            dimension_semantics=("arbitrary",), vmem_limit_bytes=48 * 1024 * 1024
        ),
        cost_estimate=pl.CostEstimate(
            flops=8 * count * elems * samples,
            transcendentals=0,
            bytes_accessed=4 * count * elems + 4 * elems * samples + 8 * count * samples,
        ),
    )(index.reshape(1), w, x)


def send_plan(n_elem):
    plan = []
    serves = []
    for step in range(1, n_elem):
        right = {c: c + n_elem - step for c in range(step)}
        left = {c: c - n_elem + step for c in range(n_elem - step, n_elem)}
        if set(right) & set(left):
            plan += [right, left]
            serves += [(step, "right"), (step, "left")]
        else:
            plan.append({**right, **left})
            serves.append((step, "both"))
    own_call = {}
    for c in range(n_elem):
        free = [k for k, row in enumerate(plan) if c not in row]
        if free:
            plan[free[0]][c] = c
            own_call[c] = free[0]
        else:
            plan.append({c: c})
            serves.append((None, "own"))
            own_call[c] = len(plan) - 1
    table = [[row.get(c, c) for c in range(n_elem)] for row in plan]
    return table, serves, own_call


def line_scatter(signal, weights, n_elem):
    me = lax.axis_index("elem")
    local = weights.shape[2] // n_elem
    table, serves, own_call = send_plan(n_elem)
    made = []
    later = jnp.asarray(table, jnp.int32)[:, me]
    for k, row in enumerate(table):
        if k == 0 and row == [n_elem - 1] + list(range(1, n_elem - 1)) + [0]:
            index = jnp.where(me == 0, n_elem - 1, jnp.where(me == n_elem - 1, 0, me)).astype(jnp.int32)
        else:
            index = later[k]
        made.append(jnp.swapaxes(block_partial(signal, weights, index, local), 1, 2))
    got_right = None
    got_left = None
    shared = False
    for step in range(1, n_elem):
        calls = {way: k for k, (s, way) in enumerate(serves) if s == step}
        to_right = made[calls.get("right", calls.get("both"))]
        to_left = made[calls.get("left", calls.get("both"))]
        if got_right is not None:
            to_right = to_right + got_right
            to_left = to_left + got_left
        pairs_right = [(c, c + 1) for c in range(step)]
        pairs_left = [(c, c - 1) for c in range(n_elem - step, n_elem)]
        merged = pairs_right + pairs_left
        if "both" in calls and got_right is None and len({t for _, t in merged}) == len(merged):
            got_right = got_left = lax.ppermute(to_right, "elem", merged)
            shared = True
        else:
            got_right = lax.ppermute(to_right, "elem", pairs_right)
            got_left = lax.ppermute(to_left, "elem", pairs_left)
            shared = False
    own_at = jnp.asarray([own_call[c] for c in range(n_elem)], jnp.int32)[me]
    used = sorted(set(own_call.values()))
    own = made[used[0]]
    for k in used[1:]:
        own = jnp.where(own_at == k, made[k], own)
    if shared:
        return own + got_right
    return own + got_right + got_left


def on_device(signal, weights):
    n_elem = lax.axis_size("elem")
    samples = signal.shape[3]
    gates = samples // PULSES
    beams = weights.shape[2]
    if n_elem in (2, 4):
        summed = line_scatter(signal, weights, n_elem)
    else:
        part = partials(signal, weights)
        summed = lax.psum_scatter(part, "elem", scatter_dimension=1, tiled=True)
    stats = beam_stats(summed, gates)
    padded = with_halo(stats, "gate", 2)
    smoothed = (padded[..., :-2] + 2.0 * padded[..., 1:-1] + padded[..., 2:]) * 0.25
    power = smoothed[0]
    magnitude = jnp.sqrt(smoothed[1] * smoothed[1] + smoothed[2] * smoothed[2])
    floor_mag = jnp.maximum(magnitude, 0.25 * power)
    moments = jnp.stack(
        [
            10.0 * jnp.log10(power + 1e-06),
            smoothed[1] / floor_mag,
            smoothed[2] / floor_mag,
            jnp.log(power / floor_mag),
        ]
    )
    zdr = 10.0 * jnp.log10((smoothed[3] + 1e-06) / (smoothed[4] + 1e-06))
    corr = jnp.sqrt(smoothed[5] * smoothed[5] + smoothed[6] * smoothed[6]) / jnp.sqrt(
        smoothed[3] * smoothed[4]
    )
    pol_index = lax.axis_index("pol")
    polar = jnp.where(pol_index == 0, zdr, corr)
    return (moments[:, None], polar[None])


def solution(mesh):
    return jax.shard_map(
        on_device,
        mesh=mesh,
        in_specs=(P("arrays", "pol", "elem", "gate"), P("arrays", "pol", None, "elem")),
        out_specs=(
            P(None, ("arrays", "pol"), "elem", "gate"),
            P("pol", ("arrays", "elem"), "gate"),
        ),
        check_vma=False,
    )
```

```python
import jax
import jax.numpy as jnp
from jax import lax
from jax.experimental import pallas as pl
from jax.experimental.pallas import tpu as pltpu
from jax.sharding import PartitionSpec as P

PULSES = 64
BEAM_TILE = 512
ELEM_TILE = 1024
FIRST_TILE = 2048


def swapped(value, axis, bit):
    mask = 2**bit
    pairs = [(source, source ^ mask) for source in range(lax.axis_size(axis))]
    return lax.ppermute(value, axis, pairs)


def with_halo(block, axis, dim):
    count = lax.axis_size(axis)
    first = lax.slice_in_dim(block, 0, 1, axis=dim)
    last = lax.slice_in_dim(block, block.shape[dim] - 1, None, axis=dim)
    index = lax.axis_index(axis)
    if count == 2:
        sent = jnp.where(index == 0, last, first)
        got = lax.ppermute(sent, axis, [(0, 1), (1, 0)])
        zero = jnp.zeros_like(got)
        low = jnp.where(index == 0, zero, got)
        high = jnp.where(index == 0, got, zero)
    else:
        forward = [(i, i + 1) for i in range(count - 1)]
        backward = [(target, source) for source, target in forward]
        low = lax.ppermute(last, axis, forward)
        high = lax.ppermute(first, axis, backward)
    return jnp.concatenate([low, block, high], axis=dim)


def lag_stats(real, imag):
    zero_lag = jnp.mean(real * real + imag * imag, axis=-1)
    lag_re = jnp.sum(real[..., :-1] * real[..., 1:] + imag[..., :-1] * imag[..., 1:], axis=-1) / (
        PULSES - 1
    )
    lag_im = jnp.sum(real[..., :-1] * imag[..., 1:] - imag[..., :-1] * real[..., 1:], axis=-1) / (
        PULSES - 1
    )
    return (zero_lag, lag_re, lag_im)


def pair_stats(first, second):
    power_h = jnp.mean(first[0] * first[0] + first[1] * first[1], axis=-1)
    power_v = jnp.mean(second[0] * second[0] + second[1] * second[1], axis=-1)
    cross_re = jnp.mean(first[0] * second[0] + first[1] * second[1], axis=-1)
    cross_im = jnp.mean(first[0] * second[1] - first[1] * second[0], axis=-1)
    return (power_h, power_v, cross_re, cross_im)


def beam_stats(summed, gates):
    count = summed.shape[1]
    real = summed[0].reshape(count, gates, PULSES)
    imag = summed[1].reshape(count, gates, PULSES)
    zero_lag, lag_re, lag_im = lag_stats(real, imag)
    series = jnp.stack([real, imag])
    pol_index = lax.axis_index("pol")
    other = swapped(series, "pol", 0)
    first = jnp.where(pol_index == 0, series, other)
    second = jnp.where(pol_index == 0, other, series)
    pair = jnp.stack(pair_stats(first, second))
    return jnp.concatenate([jnp.stack([zero_lag, lag_re, lag_im]), pair], axis=0)


def complex_kernel(half_ref, w_ref, x_ref, o_ref):
    bt = w_ref.shape[1]
    rows = w_ref[...].reshape(2 * bt, w_ref.shape[2])
    with_re = jnp.dot(rows, x_ref[0], preferred_element_type=jnp.float32)
    with_im = jnp.dot(rows, x_ref[1], preferred_element_type=jnp.float32)
    real = with_re[:bt] + with_im[bt:]
    imag = with_im[:bt] - with_re[bt:]

    @pl.when(pl.program_id(1) == 0)
    def _():
        o_ref[0] = real
        o_ref[1] = imag

    @pl.when(pl.program_id(1) > 0)
    def _():
        o_ref[0] += real
        o_ref[1] += imag


def partials(signal, weights, half=None):
    w = weights[:, 0]
    x = signal[:, 0]
    beams, elems = w.shape[1], w.shape[2]
    samples = x.shape[2]
    rows = beams if half is None else beams // 2
    bt = min(BEAM_TILE, rows)
    tk = min(ELEM_TILE, elems)
    tiles = rows // bt
    if half is None:
        half = jnp.zeros((1,), jnp.int32)
    return pl.pallas_call(
        complex_kernel,
        out_shape=jax.ShapeDtypeStruct((2, rows, samples), jnp.float32),
        grid_spec=pltpu.PrefetchScalarGridSpec(
            num_scalar_prefetch=1,
            grid=(tiles, elems // tk),
            in_specs=[
                pl.BlockSpec((2, bt, tk), lambda i, k, h: (0, h[0] * tiles + i, k)),
                pl.BlockSpec((2, tk, samples), lambda i, k, h: (0, k, 0)),
            ],
            out_specs=pl.BlockSpec((2, bt, samples), lambda i, k, h: (0, i, 0)),
        ),
        compiler_params=pltpu.CompilerParams(
            dimension_semantics=("arbitrary", "arbitrary"), vmem_limit_bytes=48 * 1024 * 1024
        ),
        cost_estimate=pl.CostEstimate(
            flops=8 * rows * elems * samples,
            transcendentals=0,
            bytes_accessed=4 * rows * elems + 4 * elems * samples * tiles + 8 * rows * samples,
        ),
    )(half, w, x)


def block_kernel(index_ref, w_ref, x_ref, o_ref, acc_ref):
    bt = w_ref.shape[1]
    rows = w_ref[...].reshape(2 * bt, w_ref.shape[2])
    with_re = jnp.dot(rows, x_ref[0], preferred_element_type=jnp.float32)
    with_im = jnp.dot(rows, x_ref[1], preferred_element_type=jnp.float32)
    real = with_re[:bt] + with_im[bt:]
    imag = with_im[:bt] - with_re[bt:]
    step = pl.program_id(0)

    @pl.when(step == 0)
    def _():
        acc_ref[0] = real
        acc_ref[1] = imag

    @pl.when(step > 0)
    def _():
        acc_ref[0] += real
        acc_ref[1] += imag

    @pl.when(step == pl.num_programs(0) - 1)
    def _():
        o_ref[0] = acc_ref[0].T
        o_ref[1] = acc_ref[1].T


def block_partial(signal, weights, index, count, tile=ELEM_TILE):
    w = weights[:, 0]
    x = signal[:, 0]
    elems = w.shape[2]
    samples = x.shape[2]
    tk = min(tile, elems)
    return pl.pallas_call(
        block_kernel,
        out_shape=jax.ShapeDtypeStruct((2, samples, count), jnp.float32),
        grid_spec=pltpu.PrefetchScalarGridSpec(
            num_scalar_prefetch=1,
            grid=(elems // tk,),
            in_specs=[
                pl.BlockSpec((2, count, tk), lambda k, b: (0, b[0], k)),
                pl.BlockSpec((2, tk, samples), lambda k, b: (0, k, 0)),
            ],
            out_specs=pl.BlockSpec((2, samples, count), lambda k, b: (0, 0, 0)),
            scratch_shapes=[pltpu.VMEM((2, count, samples), jnp.float32)],
        ),
        compiler_params=pltpu.CompilerParams(
            dimension_semantics=("arbitrary",), vmem_limit_bytes=48 * 1024 * 1024
        ),
        cost_estimate=pl.CostEstimate(
            flops=8 * count * elems * samples,
            transcendentals=0,
            bytes_accessed=4 * count * elems + 4 * elems * samples + 8 * count * samples,
        ),
    )(index.reshape(1), w, x)


def send_plan(n_elem):
    plan = []
    serves = []
    for step in range(1, n_elem):
        right = {c: c + n_elem - step for c in range(step)}
        left = {c: c - n_elem + step for c in range(n_elem - step, n_elem)}
        if set(right) & set(left):
            plan += [right, left]
            serves += [(step, "right"), (step, "left")]
        else:
            plan.append({**right, **left})
            serves.append((step, "both"))
    own_call = {}
    for c in range(n_elem):
        free = [k for k, row in enumerate(plan) if c not in row]
        if free:
            plan[free[0]][c] = c
            own_call[c] = free[0]
        else:
            plan.append({c: c})
            serves.append((None, "own"))
            own_call[c] = len(plan) - 1
    table = [[row.get(c, c) for c in range(n_elem)] for row in plan]
    return table, serves, own_call


def line_scatter(signal, weights, n_elem):
    me = lax.axis_index("elem")
    local = weights.shape[2] // n_elem
    table, serves, own_call = send_plan(n_elem)
    made = []
    later = jnp.asarray(table, jnp.int32)[:, me]
    for k, row in enumerate(table):
        if k == 0 and row == [n_elem - 1] + list(range(1, n_elem - 1)) + [0]:
            index = jnp.where(me == 0, n_elem - 1, jnp.where(me == n_elem - 1, 0, me)).astype(jnp.int32)
        else:
            index = later[k]
        tile = FIRST_TILE if k == 0 else ELEM_TILE
        made.append(jnp.swapaxes(block_partial(signal, weights, index, local, tile), 1, 2))
    got_right = None
    got_left = None
    shared = False
    for step in range(1, n_elem):
        calls = {way: k for k, (s, way) in enumerate(serves) if s == step}
        to_right = made[calls.get("right", calls.get("both"))]
        to_left = made[calls.get("left", calls.get("both"))]
        if got_right is not None:
            to_right = to_right + got_right
            to_left = to_left + got_left
        pairs_right = [(c, c + 1) for c in range(step)]
        pairs_left = [(c, c - 1) for c in range(n_elem - step, n_elem)]
        merged = pairs_right + pairs_left
        if "both" in calls and got_right is None and len({t for _, t in merged}) == len(merged):
            got_right = got_left = lax.ppermute(to_right, "elem", merged)
            shared = True
        else:
            got_right = lax.ppermute(to_right, "elem", pairs_right)
            got_left = lax.ppermute(to_left, "elem", pairs_left)
            shared = False
    own_at = jnp.asarray([own_call[c] for c in range(n_elem)], jnp.int32)[me]
    used = sorted(set(own_call.values()))
    own = made[used[0]]
    for k in used[1:]:
        own = jnp.where(own_at == k, made[k], own)
    if shared:
        return own + got_right
    return own + got_right + got_left


def on_device(signal, weights):
    n_elem = lax.axis_size("elem")
    samples = signal.shape[3]
    gates = samples // PULSES
    beams = weights.shape[2]
    if n_elem in (2, 4):
        summed = line_scatter(signal, weights, n_elem)
    else:
        part = partials(signal, weights)
        summed = lax.psum_scatter(part, "elem", scatter_dimension=1, tiled=True)
    stats = beam_stats(summed, gates)
    padded = with_halo(stats, "gate", 2)
    smoothed = (padded[..., :-2] + 2.0 * padded[..., 1:-1] + padded[..., 2:]) * 0.25
    power = smoothed[0]
    magnitude = jnp.sqrt(smoothed[1] * smoothed[1] + smoothed[2] * smoothed[2])
    floor_mag = jnp.maximum(magnitude, 0.25 * power)
    moments = jnp.stack(
        [
            10.0 * jnp.log10(power + 1e-06),
            smoothed[1] / floor_mag,
            smoothed[2] / floor_mag,
            jnp.log(power / floor_mag),
        ]
    )
    zdr = 10.0 * jnp.log10((smoothed[3] + 1e-06) / (smoothed[4] + 1e-06))
    corr = jnp.sqrt(smoothed[5] * smoothed[5] + smoothed[6] * smoothed[6]) / jnp.sqrt(
        smoothed[3] * smoothed[4]
    )
    pol_index = lax.axis_index("pol")
    polar = jnp.where(pol_index == 0, zdr, corr)
    return (moments[:, None], polar[None])


def solution(mesh):
    return jax.shard_map(
        on_device,
        mesh=mesh,
        in_specs=(P("arrays", "pol", "elem", "gate"), P("arrays", "pol", None, "elem")),
        out_specs=(
            P(None, ("arrays", "pol"), "elem", "gate"),
            P("pol", ("arrays", "elem"), "gate"),
        ),
        check_vma=False,
    )
```

```python
import jax
import jax.numpy as jnp
from jax import lax
from jax.experimental import pallas as pl
from jax.experimental.pallas import tpu as pltpu
from jax.sharding import PartitionSpec as P

PULSES = 64
BEAM_TILE = 512
ELEM_TILE = 2048
FIRST_TILE = 2048


def swapped(value, axis, bit):
    mask = 2**bit
    pairs = [(source, source ^ mask) for source in range(lax.axis_size(axis))]
    return lax.ppermute(value, axis, pairs)


def with_halo(block, axis, dim):
    count = lax.axis_size(axis)
    first = lax.slice_in_dim(block, 0, 1, axis=dim)
    last = lax.slice_in_dim(block, block.shape[dim] - 1, None, axis=dim)
    index = lax.axis_index(axis)
    if count == 2:
        sent = jnp.where(index == 0, last, first)
        got = lax.ppermute(sent, axis, [(0, 1), (1, 0)])
        zero = jnp.zeros_like(got)
        low = jnp.where(index == 0, zero, got)
        high = jnp.where(index == 0, got, zero)
    else:
        forward = [(i, i + 1) for i in range(count - 1)]
        backward = [(target, source) for source, target in forward]
        low = lax.ppermute(last, axis, forward)
        high = lax.ppermute(first, axis, backward)
    return jnp.concatenate([low, block, high], axis=dim)


def lag_stats(real, imag):
    zero_lag = jnp.mean(real * real + imag * imag, axis=-1)
    lag_re = jnp.sum(real[..., :-1] * real[..., 1:] + imag[..., :-1] * imag[..., 1:], axis=-1) / (
        PULSES - 1
    )
    lag_im = jnp.sum(real[..., :-1] * imag[..., 1:] - imag[..., :-1] * real[..., 1:], axis=-1) / (
        PULSES - 1
    )
    return (zero_lag, lag_re, lag_im)


def pair_stats(first, second):
    power_h = jnp.mean(first[0] * first[0] + first[1] * first[1], axis=-1)
    power_v = jnp.mean(second[0] * second[0] + second[1] * second[1], axis=-1)
    cross_re = jnp.mean(first[0] * second[0] + first[1] * second[1], axis=-1)
    cross_im = jnp.mean(first[0] * second[1] - first[1] * second[0], axis=-1)
    return (power_h, power_v, cross_re, cross_im)


def beam_stats(summed, gates):
    count = summed.shape[1]
    real = summed[0].reshape(count, gates, PULSES)
    imag = summed[1].reshape(count, gates, PULSES)
    zero_lag, lag_re, lag_im = lag_stats(real, imag)
    series = jnp.stack([real, imag])
    pol_index = lax.axis_index("pol")
    other = swapped(series, "pol", 0)
    first = jnp.where(pol_index == 0, series, other)
    second = jnp.where(pol_index == 0, other, series)
    pair = jnp.stack(pair_stats(first, second))
    return jnp.concatenate([jnp.stack([zero_lag, lag_re, lag_im]), pair], axis=0)


def complex_kernel(half_ref, w_ref, x_ref, o_ref):
    bt = w_ref.shape[1]
    rows = w_ref[...].reshape(2 * bt, w_ref.shape[2])
    with_re = jnp.dot(rows, x_ref[0], preferred_element_type=jnp.float32)
    with_im = jnp.dot(rows, x_ref[1], preferred_element_type=jnp.float32)
    real = with_re[:bt] + with_im[bt:]
    imag = with_im[:bt] - with_re[bt:]

    @pl.when(pl.program_id(1) == 0)
    def _():
        o_ref[0] = real
        o_ref[1] = imag

    @pl.when(pl.program_id(1) > 0)
    def _():
        o_ref[0] += real
        o_ref[1] += imag


def partials(signal, weights, half=None):
    w = weights[:, 0]
    x = signal[:, 0]
    beams, elems = w.shape[1], w.shape[2]
    samples = x.shape[2]
    rows = beams if half is None else beams // 2
    bt = min(BEAM_TILE, rows)
    tk = min(ELEM_TILE, elems)
    tiles = rows // bt
    if half is None:
        half = jnp.zeros((1,), jnp.int32)
    return pl.pallas_call(
        complex_kernel,
        out_shape=jax.ShapeDtypeStruct((2, rows, samples), jnp.float32),
        grid_spec=pltpu.PrefetchScalarGridSpec(
            num_scalar_prefetch=1,
            grid=(tiles, elems // tk),
            in_specs=[
                pl.BlockSpec((2, bt, tk), lambda i, k, h: (0, h[0] * tiles + i, k)),
                pl.BlockSpec((2, tk, samples), lambda i, k, h: (0, k, 0)),
            ],
            out_specs=pl.BlockSpec((2, bt, samples), lambda i, k, h: (0, i, 0)),
        ),
        compiler_params=pltpu.CompilerParams(
            dimension_semantics=("arbitrary", "arbitrary"), vmem_limit_bytes=48 * 1024 * 1024
        ),
        cost_estimate=pl.CostEstimate(
            flops=8 * rows * elems * samples,
            transcendentals=0,
            bytes_accessed=4 * rows * elems + 4 * elems * samples * tiles + 8 * rows * samples,
        ),
    )(half, w, x)


def block_kernel(index_ref, w_ref, x_ref, o_ref, acc_ref):
    bt = w_ref.shape[1]
    rows = w_ref[...].reshape(2 * bt, w_ref.shape[2])
    with_re = jnp.dot(rows, x_ref[0], preferred_element_type=jnp.float32)
    with_im = jnp.dot(rows, x_ref[1], preferred_element_type=jnp.float32)
    real = with_re[:bt] + with_im[bt:]
    imag = with_im[:bt] - with_re[bt:]
    step = pl.program_id(0)

    @pl.when(step == 0)
    def _():
        acc_ref[0] = real
        acc_ref[1] = imag

    @pl.when(step > 0)
    def _():
        acc_ref[0] += real
        acc_ref[1] += imag

    @pl.when(step == pl.num_programs(0) - 1)
    def _():
        o_ref[0] = acc_ref[0].T
        o_ref[1] = acc_ref[1].T


def block_partial(signal, weights, index, count, tile=ELEM_TILE):
    w = weights[:, 0]
    x = signal[:, 0]
    elems = w.shape[2]
    samples = x.shape[2]
    tk = min(tile, elems)
    return pl.pallas_call(
        block_kernel,
        out_shape=jax.ShapeDtypeStruct((2, samples, count), jnp.float32),
        grid_spec=pltpu.PrefetchScalarGridSpec(
            num_scalar_prefetch=1,
            grid=(elems // tk,),
            in_specs=[
                pl.BlockSpec((2, count, tk), lambda k, b: (0, b[0], k)),
                pl.BlockSpec((2, tk, samples), lambda k, b: (0, k, 0)),
            ],
            out_specs=pl.BlockSpec((2, samples, count), lambda k, b: (0, 0, 0)),
            scratch_shapes=[pltpu.VMEM((2, count, samples), jnp.float32)],
        ),
        compiler_params=pltpu.CompilerParams(
            dimension_semantics=("arbitrary",), vmem_limit_bytes=48 * 1024 * 1024
        ),
        cost_estimate=pl.CostEstimate(
            flops=8 * count * elems * samples,
            transcendentals=0,
            bytes_accessed=4 * count * elems + 4 * elems * samples + 8 * count * samples,
        ),
    )(index.reshape(1), w, x)


def send_plan(n_elem):
    plan = []
    serves = []
    for step in range(1, n_elem):
        right = {c: c + n_elem - step for c in range(step)}
        left = {c: c - n_elem + step for c in range(n_elem - step, n_elem)}
        if set(right) & set(left):
            plan += [right, left]
            serves += [(step, "right"), (step, "left")]
        else:
            plan.append({**right, **left})
            serves.append((step, "both"))
    own_call = {}
    for c in range(n_elem):
        free = [k for k, row in enumerate(plan) if c not in row]
        if free:
            plan[free[0]][c] = c
            own_call[c] = free[0]
        else:
            plan.append({c: c})
            serves.append((None, "own"))
            own_call[c] = len(plan) - 1
    table = [[row.get(c, c) for c in range(n_elem)] for row in plan]
    return table, serves, own_call


def line_scatter(signal, weights, n_elem):
    me = lax.axis_index("elem")
    local = weights.shape[2] // n_elem
    table, serves, own_call = send_plan(n_elem)
    made = []
    later = jnp.asarray(table, jnp.int32)[:, me]
    for k, row in enumerate(table):
        if k == 0 and row == [n_elem - 1] + list(range(1, n_elem - 1)) + [0]:
            index = jnp.where(me == 0, n_elem - 1, jnp.where(me == n_elem - 1, 0, me)).astype(jnp.int32)
        else:
            index = later[k]
        tile = FIRST_TILE if k == 0 else ELEM_TILE
        made.append(jnp.swapaxes(block_partial(signal, weights, index, local, tile), 1, 2))
    got_right = None
    got_left = None
    shared = False
    for step in range(1, n_elem):
        calls = {way: k for k, (s, way) in enumerate(serves) if s == step}
        to_right = made[calls.get("right", calls.get("both"))]
        to_left = made[calls.get("left", calls.get("both"))]
        if got_right is not None:
            to_right = to_right + got_right
            to_left = to_left + got_left
        pairs_right = [(c, c + 1) for c in range(step)]
        pairs_left = [(c, c - 1) for c in range(n_elem - step, n_elem)]
        merged = pairs_right + pairs_left
        if "both" in calls and got_right is None and len({t for _, t in merged}) == len(merged):
            got_right = got_left = lax.ppermute(to_right, "elem", merged)
            shared = True
        else:
            got_right = lax.ppermute(to_right, "elem", pairs_right)
            got_left = lax.ppermute(to_left, "elem", pairs_left)
            shared = False
    own_at = jnp.asarray([own_call[c] for c in range(n_elem)], jnp.int32)[me]
    used = sorted(set(own_call.values()))
    own = made[used[0]]
    for k in used[1:]:
        own = jnp.where(own_at == k, made[k], own)
    if shared:
        return own + got_right
    return own + got_right + got_left


def on_device(signal, weights):
    n_elem = lax.axis_size("elem")
    samples = signal.shape[3]
    gates = samples // PULSES
    beams = weights.shape[2]
    if n_elem in (2, 4):
        summed = line_scatter(signal, weights, n_elem)
    else:
        part = partials(signal, weights)
        summed = lax.psum_scatter(part, "elem", scatter_dimension=1, tiled=True)
    stats = beam_stats(summed, gates)
    padded = with_halo(stats, "gate", 2)
    smoothed = (padded[..., :-2] + 2.0 * padded[..., 1:-1] + padded[..., 2:]) * 0.25
    power = smoothed[0]
    magnitude = jnp.sqrt(smoothed[1] * smoothed[1] + smoothed[2] * smoothed[2])
    floor_mag = jnp.maximum(magnitude, 0.25 * power)
    moments = jnp.stack(
        [
            10.0 * jnp.log10(power + 1e-06),
            smoothed[1] / floor_mag,
            smoothed[2] / floor_mag,
            jnp.log(power / floor_mag),
        ]
    )
    zdr = 10.0 * jnp.log10((smoothed[3] + 1e-06) / (smoothed[4] + 1e-06))
    corr = jnp.sqrt(smoothed[5] * smoothed[5] + smoothed[6] * smoothed[6]) / jnp.sqrt(
        smoothed[3] * smoothed[4]
    )
    pol_index = lax.axis_index("pol")
    polar = jnp.where(pol_index == 0, zdr, corr)
    return (moments[:, None], polar[None])


def solution(mesh):
    return jax.shard_map(
        on_device,
        mesh=mesh,
        in_specs=(P("arrays", "pol", "elem", "gate"), P("arrays", "pol", None, "elem")),
        out_specs=(
            P(None, ("arrays", "pol"), "elem", "gate"),
            P("pol", ("arrays", "elem"), "gate"),
        ),
        check_vma=False,
    )
```
